128 devices in a mesh: req: 8 (over x, core), hid: 16 (over z, y).
Axes of the slice: x: 4, y: 4, z: 4, core: 2. Of those that a mesh axis runs over, the one named last changes fastest.
Arguments:
- queries: bfloat16 [16, 128, 8192], P('req', None, 'hid'), may hold values from -400 to 400
- suffix_keys: bfloat16 [16, 128, 1024], P('req'), may hold values from -6 to 6
- suffix_values: bfloat16 [16, 128, 1024], P('req'), may hold values from -6 to 6
- prefix_cache: bfloat16 [8192, 2, 1024], P('req'), may hold values from -6 to 6
- prefix_block: int32 [32], replicated, may hold values from 0 to 31, each once
- suffix_len: int32 [16], replicated, may hold values from 1 to 128, 1024 in all
- slot_request: int32 [16], replicated, may hold values from 0 to 15, each once
- residual: bfloat16 [1024, 8192], P(None, 'req'), may hold values from -10 to 10
- out_weight: bfloat16 [8192, 8192], P('hid', 'req'), may hold values from -10 to 10
- post_gain: float32 [8192], P('req'), may hold values from 0.1 to 1.9
- gate_weight: bfloat16 [8192, 28672], P('req', 'hid'), may hold values from -0.0625 to 0.0625
- up_weight: bfloat16 [8192, 28672], P('req', 'hid'), may hold values from -0.0625 to 0.0625
- down_weight: bfloat16 [28672, 8192], P('hid', 'req'), may hold values from -0.03125 to 0.03125
Outputs:
- mixed: bfloat16 [1024, 8192], P('hid', 'req')
The draws below stay inside these ranges and needn't reach their ends.
Inputs may be any that keep to these rules, and one draw needn't show every extreme that they name: Request i has suffix_len[i] new tokens; they sum to 1024, and the longest has exactly 128. Slot s holds request slot_request[s]; slots r * 2 to (r + 1) * 2 - 1 lie on req index r; every request stands in one slot. Storage rows i * 256 to (i + 1) * 256 - 1 of prefix_cache hold prefix block prefix_block[i]; every block is stored once.
All inputs are finite; a program needn't handle non-finite values.
Results may differ from the reference program's by a relative error of at most 0.019.
Values may be sent and summed in bfloat16 or wider, within the bound.
No kernel may reach another device: no remote copies, remote signals or barrier semaphores. Data moves between devices by JAX's collectives and lax.ppermute only.
A program may use at most 128 MiB of HBM per device.

```python
import math
import jax
import jax.numpy as jnp
import numpy as np
from jax import lax

D = 8192
H = 64
KVH = 8
HD = 128
FF = 28672
PREFIX = 8192
PBLK = 256
MAXLEN = 128
NREQ = 16
TOKENS = 1024
NPB = 32
N_REQ = 8


def draw_queries(key, part):
    base_key = jax.random.fold_in(key, 11)
    normal_part = jnp.clip(jax.random.normal(base_key, (NREQ, MAXLEN, H * HD), jnp.float32), -5.0, 5.0)
    return normal_part.astype(jnp.bfloat16)


def width_ramp(low_end, high_end):
    column = jnp.arange(D, dtype=jnp.float32) / (D - 1.0)
    return low_end * jnp.exp(jnp.log(high_end / low_end) * column)


def draw_residual(key, part):
    base_key = jax.random.fold_in(key, 21)
    values = jnp.clip(jax.random.normal(base_key, (TOKENS, D), jnp.float32), -5.0, 5.0)
    return (values * width_ramp(0.3, 1.8)[None, :]).astype(jnp.bfloat16)


def draw_out_weight(key, part):
    base_key = jax.random.fold_in(key, 31)
    fan_scale = (H * HD / 256.0) ** (-0.5)
    values = jnp.clip(jax.random.normal(base_key, (H * HD, D), jnp.float32), -5.0, 5.0)
    return (values * fan_scale * width_ramp(0.3, 1.8)[None, :]).astype(jnp.bfloat16)


def steps_of(key, shape, cuts, low, largest):
    level, own = 1.0, jax.random.fold_in(key, 6)
    for axis_at, parts in cuts:
        heights = jnp.exp(jax.random.uniform(jax.random.fold_in(own, axis_at), (parts,), jnp.float32, low / len(cuts), largest / len(cuts)))
        level = level * jnp.repeat(heights, shape[axis_at] // parts).reshape([-1 if axis == axis_at else 1 for axis in range(len(shape))])
    return level


def split_up(amount, total, reach, skew):
    loads = [(1 << 20) // math.isqrt(rank ** skew) + 1 for rank in range(2, amount + 1)]
    spare, holding = total - reach - (amount - 1), [1] * (amount - 1)
    while spare > 0:
        movable = [i for i in range(amount - 1) if holding[i] < reach]
        pool, remaining = sum([loads[i] for i in movable]), spare
        for i in movable:
            more = min(reach - holding[i], max(1, remaining * loads[i] // pool), spare)
            holding[i] = holding[i] + more
            spare = spare - more
    return np.array([reach] + holding)


def uneven_parts(own_key, number_of, total, limit, skew):
    if number_of == 2:
        one = jax.random.randint(own_key, (), max(1, total - limit), min(limit, total - 1) + 1)
        return jnp.stack([one, total - one])
    tallies = jnp.asarray(split_up(number_of, total, limit, skew), jnp.int32)
    twos = (number_of - 1) // 2
    giver, sink = tallies[1:1 + 2 * twos:2], tallies[2:2 + 2 * twos:2]
    margin = jnp.minimum(giver - 1, limit - sink)
    moved = jax.random.randint(jax.random.fold_in(own_key, 1), (twos,), 0, 1 << 20) % (margin + 1)
    tallies = tallies.at[1:1 + 2 * twos:2].set(giver - moved).at[2:2 + 2 * twos:2].set(sink + moved)
    return tallies[jax.random.permutation(jax.random.fold_in(own_key, 2), number_of)]


def centred(own_key, extent, deviation, most, shards=(), held_as=jnp.bfloat16):
    drawn = jax.random.normal(own_key, extent, jnp.float32) * deviation
    if len(shards) > 0:
        drawn = steps_of(own_key, extent, shards, -0.22, 0.18) * drawn
    return jnp.clip(drawn, min=-most, max=most).astype(held_as)


def setup_inputs(seed: int = 0) -> dict:
    streams_of = jax.random.split(jax.random.key(seed), 14)
    return {
        "queries": draw_queries(jax.random.fold_in(streams_of[13], 71), 0),
        "suffix_keys": centred(streams_of[1], (NREQ, MAXLEN, KVH * HD), 1.0, 6.0, ((0, 8),)),
        "suffix_values": centred(streams_of[2], (NREQ, MAXLEN, KVH * HD), 1.0, 6.0, ((0, 8),)),
        "prefix_cache": centred(streams_of[3], (PREFIX, 2, KVH * HD), 1.0, 6.0, ((0, 8),)),
        "prefix_block": jax.random.permutation(streams_of[4], NPB).astype(jnp.int32),
        "suffix_len": uneven_parts(streams_of[5], NREQ, TOKENS, MAXLEN, 2).astype(jnp.int32),
        "slot_request": jax.random.permutation(streams_of[6], NREQ).astype(jnp.int32),
        "residual": draw_residual(jax.random.fold_in(streams_of[13], 71), 0),
        "out_weight": draw_out_weight(jax.random.fold_in(streams_of[13], 71), 0),
        "post_gain": jnp.clip(1.0 + 0.18 * jax.random.normal(streams_of[9], (D,), jnp.float32), 0.1, 1.9),
        "gate_weight": centred(streams_of[10], (D, FF), D ** -0.5, 0.0625, ((0, 8), (1, 16))),
        "up_weight": centred(streams_of[11], (D, FF), D ** -0.5, 0.0625, ((0, 8), (1, 16))),
        "down_weight": centred(streams_of[12], (FF, D), FF ** -0.5, 0.03125, ((0, 16), (1, 8))),
    }


ROPE_BASE = 500000.0
EPSILON = 1e-05
MASKED = -1e+30

def rounded(values):
    return lax.optimization_barrier(values.astype(jnp.bfloat16)).astype(jnp.float32)

def rotate(vectors, positions):
    half_width = vectors.shape[-1] // 2
    exponent = 2.0 * jnp.arange(half_width, dtype=jnp.float32) / vectors.shape[-1]
    frequency = jnp.exp(-jnp.log(ROPE_BASE) * exponent)
    angles = positions[..., None] * frequency
    cosine = jnp.cos(angles)
    sine_part = jnp.sin(angles)
    lower_half = vectors[..., :half_width]
    upper_half = vectors[..., half_width:]
    return jnp.concatenate([lower_half * cosine - upper_half * sine_part, upper_half * cosine + lower_half * sine_part], axis=-1)

def slot_lengths(suffix_len, slot_request):
    total_count = suffix_len.shape[0]
    matches = (slot_request[:, None] == jnp.arange(total_count, dtype=jnp.int32)[None, :]).astype(jnp.int32)
    return lax.optimization_barrier(jnp.sum(matches * suffix_len[None, :], axis=1))

def token_source(suffix_len, slot_request, tokens, maxlen):
    total_count = suffix_len.shape[0]
    numbers = jnp.arange(total_count, dtype=jnp.int32)
    starts = jnp.cumsum(suffix_len).astype(jnp.int32) - suffix_len
    token_ids = jnp.arange(tokens, dtype=jnp.int32)
    reached = (token_ids[:, None] >= starts[None, :]).astype(jnp.int32)
    owner_req = lax.optimization_barrier(jnp.sum(reached, axis=1)) - 1
    onehot = (owner_req[:, None] == numbers[None, :]).astype(jnp.int32)
    start_tok = lax.optimization_barrier(jnp.sum(onehot * starts[None, :], axis=1))
    inverse = lax.optimization_barrier(jnp.sum((slot_request[:, None] == numbers[None, :]).astype(jnp.int32) * numbers[:, None], axis=0))
    slot_tok = lax.optimization_barrier(jnp.sum(onehot * inverse[None, :], axis=1))
    return (slot_tok * maxlen + token_ids - start_tok).astype(jnp.int32)

def reference(queries, suffix_keys, suffix_values, prefix_cache, prefix_block, suffix_len, slot_request, residual, out_weight, post_gain, gate_weight, up_weight, down_weight):
    slot_total, maxlen, query_cols = queries.shape
    prefix_rows = prefix_cache.shape[0]
    row_ids = jnp.arange(prefix_rows, dtype=jnp.int32)
    pre_pos = (prefix_block[row_ids // PBLK] * PBLK + row_ids % PBLK).astype(jnp.float32)
    pre_keys = rounded(rotate(prefix_cache[:, 0].astype(jnp.float32).reshape(prefix_rows, KVH, HD), pre_pos[:, None]))
    pre_values = prefix_cache[:, 1].astype(jnp.float32).reshape(prefix_rows, KVH, HD)
    places = jnp.arange(maxlen, dtype=jnp.int32)
    suffix_pos = (PREFIX + places).astype(jnp.float32)
    query_rot = rounded(rotate(queries.astype(jnp.float32).reshape(slot_total, maxlen, H, HD), suffix_pos[None, :, None]))
    key_rot = rounded(rotate(suffix_keys.astype(jnp.float32).reshape(slot_total, maxlen, KVH, HD), suffix_pos[None, :, None]))
    value_heads = suffix_values.astype(jnp.float32).reshape(slot_total, maxlen, KVH, HD)
    lengths_slot = slot_lengths(suffix_len, slot_request)
    allowed = (places[None, :, None] >= places[None, None, :]) & (places[None, None, :] < lengths_slot[:, None, None])
    group = H // KVH
    scale = HD ** (-0.5)

    def head_group(kv_head):
        query_part = lax.dynamic_slice_in_dim(query_rot, kv_head * group, group, 2)
        key_pre = lax.dynamic_index_in_dim(pre_keys, kv_head, 1, keepdims=False)
        value_pre = lax.dynamic_index_in_dim(pre_values, kv_head, 1, keepdims=False)
        key_suf = lax.dynamic_index_in_dim(key_rot, kv_head, 2, keepdims=False)
        value_suf = lax.dynamic_index_in_dim(value_heads, kv_head, 2, keepdims=False)
        pre_scores = jnp.einsum('stnd,pd->stnp', query_part, key_pre) * scale
        suf_scores = jnp.einsum('stnd,sud->stnu', query_part, key_suf) * scale
        suf_scores = jnp.where(allowed[:, :, None, :], suf_scores, MASKED)
        row_max = jnp.maximum(lax.optimization_barrier(jnp.max(pre_scores, axis=-1)), lax.optimization_barrier(jnp.max(suf_scores, axis=-1)))
        pre_prob = jnp.exp(pre_scores - row_max[..., None])
        suf_prob = jnp.exp(suf_scores - row_max[..., None])
        total = lax.optimization_barrier(jnp.sum(pre_prob, axis=-1)) + lax.optimization_barrier(jnp.sum(suf_prob, axis=-1))
        weighted = jnp.einsum('stnp,pd->stnd', rounded(pre_prob), value_pre)
        weighted = weighted + jnp.einsum('stnu,sud->stnd', rounded(suf_prob), value_suf)
        return (weighted / total[..., None]).astype(jnp.bfloat16)
    heads_out = lax.map(head_group, jnp.arange(KVH, dtype=jnp.int32))
    attention = jnp.transpose(heads_out, (1, 2, 0, 3, 4)).reshape(slot_total * maxlen, H * HD)
    tokens = residual.shape[0]
    source = token_source(suffix_len, slot_request, tokens, maxlen)
    projected = jnp.dot(attention[source], out_weight, preferred_element_type=jnp.float32)
    resid_f = rounded(residual.astype(jnp.float32) + projected)
    squares = lax.optimization_barrier(jnp.sum(resid_f * resid_f, axis=1))
    inv_rms = lax.rsqrt(squares / D + EPSILON)
    scaled = (resid_f * post_gain[None, :]).astype(jnp.bfloat16)
    block_width = D // N_REQ
    gate_acc = jnp.zeros((tokens, gate_weight.shape[1]), jnp.float32)
    up_acc = jnp.zeros((tokens, up_weight.shape[1]), jnp.float32)
    for block in range(N_REQ):
        scaled_block = scaled[:, block * block_width:(block + 1) * block_width]
        gate_acc = gate_acc + rounded(jnp.dot(scaled_block, gate_weight[block * block_width:(block + 1) * block_width], preferred_element_type=jnp.float32))
        up_acc = up_acc + rounded(jnp.dot(scaled_block, up_weight[block * block_width:(block + 1) * block_width], preferred_element_type=jnp.float32))
    gate_val = gate_acc * inv_rms[:, None]
    up_val = up_acc * inv_rms[:, None]
    hidden = (jax.nn.silu(gate_val) * up_val).astype(jnp.bfloat16)
    return (resid_f + jnp.dot(hidden, down_weight, preferred_element_type=jnp.float32)).astype(jnp.bfloat16)
```

```python
import jax
import jax.numpy as jnp
from jax import lax
from jax.sharding import PartitionSpec as P

D = 8192
KVH = 8
HD = 128
PREFIX = 8192
PBLK = 256


ROPE_BASE = 500000.0
EPSILON = 1e-05
MASKED = -1e30


def rotate(vectors, positions):
    half_width = vectors.shape[-1] // 2
    exponent = 2.0 * jnp.arange(half_width, dtype=jnp.float32) / vectors.shape[-1]
    frequency = jnp.exp(-jnp.log(ROPE_BASE) * exponent)
    angles = positions[..., None] * frequency
    cosine = jnp.cos(angles)
    sine_part = jnp.sin(angles)
    lower_half = vectors[..., :half_width]
    upper_half = vectors[..., half_width:]
    return jnp.concatenate(
        [
            lower_half * cosine - upper_half * sine_part,
            upper_half * cosine + lower_half * sine_part,
        ],
        axis=-1,
    )


def slot_lengths(suffix_len, slot_request):
    total_count = suffix_len.shape[0]
    matches = (slot_request[:, None] == jnp.arange(total_count, dtype=jnp.int32)[None, :]).astype(
        jnp.int32
    )
    return jnp.sum(matches * suffix_len[None, :], axis=1)


def token_source(suffix_len, slot_request, tokens, maxlen):
    total_count = suffix_len.shape[0]
    numbers = jnp.arange(total_count, dtype=jnp.int32)
    starts = jnp.cumsum(suffix_len) - suffix_len
    token_ids = jnp.arange(tokens, dtype=jnp.int32)
    reached = (token_ids[:, None] >= starts[None, :]).astype(jnp.int32)
    owner_req = jnp.sum(reached, axis=1) - 1
    onehot = (owner_req[:, None] == numbers[None, :]).astype(jnp.int32)
    start_tok = jnp.sum(onehot * starts[None, :], axis=1)
    inverse = jnp.sum(
        (slot_request[:, None] == numbers[None, :]).astype(jnp.int32) * numbers[:, None], axis=0
    )
    slot_tok = jnp.sum(onehot * inverse[None, :], axis=1)
    return slot_tok * maxlen + token_ids - start_tok


def merge_states(state_one, state_two):
    max_one, total_one, acc_one = state_one
    max_two, total_two, acc_two = state_two
    new_max = jnp.maximum(max_one, max_two)
    shrink_one = jnp.exp(max_one - new_max)
    shrink_two = jnp.exp(max_two - new_max)
    new_total = total_one * shrink_one + total_two * shrink_two
    new_acc = acc_one * shrink_one[:, None] + acc_two * shrink_two[:, None]
    return (new_max, new_total, new_acc)


def exchange_sum(values, axis, count):
    parts = lax.all_to_all(
        values.reshape(count, values.shape[0] // count, values.shape[1]), axis, 0, 0, tiled=True
    )
    return jnp.sum(parts.astype(jnp.float32), axis=0)


def exchange_gather(values, axis, count):
    parts = lax.all_to_all(
        jnp.broadcast_to(values[None], (count,) + values.shape), axis, 0, 0, tiled=True
    )
    return parts.reshape(count * values.shape[0], values.shape[1])


def on_device(
    queries,
    suffix_keys,
    suffix_values,
    prefix_cache,
    prefix_block,
    suffix_len,
    slot_request,
    residual,
    out_weight,
    post_gain,
    gate_weight,
    up_weight,
    down_weight,
):
    hid_count = lax.axis_size("hid")
    req_count = lax.axis_size("req")
    req_index = lax.axis_index("req")
    hid_index = lax.axis_index("hid")
    local_slots, maxlen, query_cols = queries.shape
    head_count = query_cols // HD
    kv_head = hid_index // (hid_count // KVH)
    scale = HD ** (-0.5)
    all_rows = local_slots * maxlen * head_count
    places = jnp.arange(maxlen, dtype=jnp.int32)
    suffix_pos = (PREFIX + places).astype(jnp.float32)
    query_rot = rotate(
        queries.astype(jnp.float32).reshape(local_slots, maxlen, head_count, HD),
        suffix_pos[None, :, None],
    ).astype(jnp.bfloat16)
    key_cols = lax.dynamic_slice_in_dim(suffix_keys, kv_head * HD, HD, 2)
    key_rot = rotate(key_cols.astype(jnp.float32), suffix_pos[None, :]).astype(jnp.bfloat16)
    value_cols = lax.dynamic_slice_in_dim(suffix_values, kv_head * HD, HD, 2)
    lengths_all = slot_lengths(suffix_len, slot_request)
    local_len = lax.dynamic_slice_in_dim(lengths_all, req_index * local_slots, local_slots, 0)
    allowed = (places[None, :, None] >= places[None, None, :]) & (
        places[None, None, :] < local_len[:, None, None]
    )
    suffix_scores = (
        jnp.einsum("jthd,jud->jthu", query_rot, key_rot, preferred_element_type=jnp.float32) * scale
    )
    suffix_scores = jnp.where(allowed[:, :, None, :], suffix_scores, MASKED)
    suffix_max = jnp.max(suffix_scores, axis=-1)
    suffix_prob = jnp.exp(suffix_scores - suffix_max[..., None])
    suffix_total = jnp.sum(suffix_prob, axis=-1)
    suffix_acc = jnp.einsum(
        "jthu,jud->jthd",
        suffix_prob.astype(jnp.bfloat16),
        value_cols,
        preferred_element_type=jnp.float32,
    )
    suffix_state = (
        suffix_max.reshape(all_rows),
        suffix_total.reshape(all_rows),
        suffix_acc.reshape(all_rows, HD),
    )
    local_prefix = prefix_cache.shape[0]
    block_count = prefix_block.shape[0]
    row_ids = req_index * local_prefix + jnp.arange(local_prefix, dtype=jnp.int32)
    block_match = (
        (row_ids // PBLK)[:, None] == jnp.arange(block_count, dtype=jnp.int32)[None, :]
    ).astype(jnp.int32)
    logical_block = jnp.sum(block_match * prefix_block[None, :], axis=1)
    pre_pos = (logical_block * PBLK + row_ids % PBLK).astype(jnp.float32)
    pre_keys = rotate(
        lax.dynamic_slice_in_dim(prefix_cache[:, 0], kv_head * HD, HD, 1).astype(jnp.float32),
        pre_pos,
    ).astype(jnp.bfloat16)
    pre_values = lax.dynamic_slice_in_dim(prefix_cache[:, 1], kv_head * HD, HD, 1)
    query_flat = query_rot.reshape(all_rows, HD)
    run_max = jnp.full((all_rows,), MASKED, jnp.float32)
    keys_piece = lax.all_gather(pre_keys, "req", axis=0, tiled=True)
    values_piece = lax.all_gather(pre_values, "req", axis=0, tiled=True)
    scores = (
        jnp.einsum("rd,pd->rp", query_flat, keys_piece, preferred_element_type=jnp.float32) * scale
    )
    new_max = jnp.maximum(run_max, jnp.max(scores, axis=1))
    probs = jnp.exp(scores - new_max[:, None])
    new_total = jnp.sum(probs, axis=1)
    new_acc = jnp.dot(probs.astype(jnp.bfloat16), values_piece, preferred_element_type=jnp.float32)
    final_state = (new_max, new_total, new_acc)
    final_state = merge_states(final_state, suffix_state)
    final_max, final_total, final_acc = final_state
    attn_local = (
        (final_acc / final_total[:, None])
        .astype(jnp.bfloat16)
        .reshape(local_slots * maxlen, head_count * HD)
    )
    dealt_rows = jnp.dot(
        lax.all_gather(attn_local, "req", axis=0, tiled=True),
        out_weight,
        preferred_element_type=jnp.float32,
    )
    tokens = residual.shape[0]
    own_rows = tokens // hid_count
    source = token_source(suffix_len, slot_request, tokens, maxlen)
    summed = exchange_sum(
        jnp.take(dealt_rows, source, axis=0).astype(jnp.bfloat16), "hid", hid_count
    )
    residual_own = lax.dynamic_slice_in_dim(residual, hid_index * own_rows, own_rows, 0)
    resid_own = (residual_own.astype(jnp.float32) + summed).astype(jnp.bfloat16)
    resid_all = exchange_gather(resid_own, "hid", hid_count)
    resid_f = lax.optimization_barrier(resid_all).astype(jnp.float32)
    squares = jnp.sum(resid_f * resid_f, axis=1)
    scaled = (resid_f * post_gain[None, :]).astype(jnp.bfloat16)
    gate_part = jnp.dot(scaled, gate_weight, preferred_element_type=jnp.float32)
    up_part = jnp.dot(scaled, up_weight, preferred_element_type=jnp.float32)
    square_all = lax.psum(squares, "req")
    gate_sum, up_sum = (
        lax.psum_scatter(
            gate_part.astype(jnp.bfloat16), "req", scatter_dimension=0, tiled=True
        ).astype(jnp.float32),
        lax.psum_scatter(
            up_part.astype(jnp.bfloat16), "req", scatter_dimension=0, tiled=True
        ).astype(jnp.float32),
    )
    row_count = tokens // req_count
    square_sum = lax.dynamic_slice_in_dim(square_all, req_index * row_count, row_count, 0)
    inv_rms = lax.rsqrt(square_sum / D + EPSILON)
    hidden = (jax.nn.silu(gate_sum * inv_rms[:, None]) * (up_sum * inv_rms[:, None])).astype(
        jnp.bfloat16
    )
    hidden_all = lax.all_gather(hidden, "req", axis=0, tiled=True)
    mixed_rows = exchange_sum(
        jnp.dot(hidden_all, down_weight, preferred_element_type=jnp.float32).astype(jnp.bfloat16),
        "hid",
        hid_count,
    )
    return (resid_own.astype(jnp.float32) + mixed_rows).astype(jnp.bfloat16)


def solution(mesh):
    return jax.shard_map(
        on_device,
        mesh=mesh,
        in_specs=(
            P("req", None, "hid"),
            P("req", None, None),
            P("req", None, None),
            P("req", None, None),
            P(),
            P(),
            P(),
            P(None, "req"),
            P("hid", "req"),
            P("req"),
            P("req", "hid"),
            P("req", "hid"),
            P("hid", "req"),
        ),
        out_specs=P("hid", "req"),
        check_vma=False,
    )
```

```python
import jax
import jax.numpy as jnp
from jax import lax
from jax.sharding import PartitionSpec as P

D = 8192
KVH = 8
HD = 128
PREFIX = 8192
PBLK = 256


ROPE_BASE = 500000.0
EPSILON = 1e-05
MASKED = -1e30


def rotate(vectors, positions):
    half_width = vectors.shape[-1] // 2
    exponent = 2.0 * jnp.arange(half_width, dtype=jnp.float32) / vectors.shape[-1]
    frequency = jnp.exp(-jnp.log(ROPE_BASE) * exponent)
    angles = positions[..., None] * frequency
    cosine = jnp.cos(angles)
    sine_part = jnp.sin(angles)
    lower_half = vectors[..., :half_width]
    upper_half = vectors[..., half_width:]
    return jnp.concatenate(
        [
            lower_half * cosine - upper_half * sine_part,
            upper_half * cosine + lower_half * sine_part,
        ],
        axis=-1,
    )


def slot_lengths(suffix_len, slot_request):
    total_count = suffix_len.shape[0]
    matches = (slot_request[:, None] == jnp.arange(total_count, dtype=jnp.int32)[None, :]).astype(
        jnp.int32
    )
    return jnp.sum(matches * suffix_len[None, :], axis=1)


def token_source(suffix_len, slot_request, tokens, maxlen):
    total_count = suffix_len.shape[0]
    numbers = jnp.arange(total_count, dtype=jnp.int32)
    starts = jnp.cumsum(suffix_len) - suffix_len
    token_ids = jnp.arange(tokens, dtype=jnp.int32)
    reached = (token_ids[:, None] >= starts[None, :]).astype(jnp.int32)
    owner_req = jnp.sum(reached, axis=1) - 1
    onehot = (owner_req[:, None] == numbers[None, :]).astype(jnp.int32)
    start_tok = jnp.sum(onehot * starts[None, :], axis=1)
    inverse = jnp.sum(
        (slot_request[:, None] == numbers[None, :]).astype(jnp.int32) * numbers[:, None], axis=0
    )
    slot_tok = jnp.sum(onehot * inverse[None, :], axis=1)
    return slot_tok * maxlen + token_ids - start_tok


def merge_states(state_one, state_two):
    max_one, total_one, acc_one = state_one
    max_two, total_two, acc_two = state_two
    new_max = jnp.maximum(max_one, max_two)
    shrink_one = jnp.exp(max_one - new_max)
    shrink_two = jnp.exp(max_two - new_max)
    new_total = total_one * shrink_one + total_two * shrink_two
    new_acc = acc_one * shrink_one[:, None] + acc_two * shrink_two[:, None]
    return (new_max, new_total, new_acc)


def exchange_sum(values, axis, count):
    parts = lax.all_to_all(
        values.reshape(count, values.shape[0] // count, values.shape[1]), axis, 0, 0, tiled=True
    )
    return jnp.sum(parts.astype(jnp.float32), axis=0)


def exchange_gather(values, axis, count):
    parts = lax.all_to_all(
        jnp.broadcast_to(values[None], (count,) + values.shape), axis, 0, 0, tiled=True
    )
    return parts.reshape(count * values.shape[0], values.shape[1])


def on_device(
    queries,
    suffix_keys,
    suffix_values,
    prefix_cache,
    prefix_block,
    suffix_len,
    slot_request,
    residual,
    out_weight,
    post_gain,
    gate_weight,
    up_weight,
    down_weight,
):
    hid_count = lax.axis_size("hid")
    req_count = lax.axis_size("req")
    req_index = lax.axis_index("req")
    hid_index = lax.axis_index("hid")
    local_slots, maxlen, query_cols = queries.shape
    head_count = query_cols // HD
    kv_head = hid_index // (hid_count // KVH)
    scale = HD ** (-0.5)
    all_rows = local_slots * maxlen * head_count
    places = jnp.arange(maxlen, dtype=jnp.int32)
    suffix_pos = (PREFIX + places).astype(jnp.float32)
    query_rot = rotate(
        queries.astype(jnp.float32).reshape(local_slots, maxlen, head_count, HD),
        suffix_pos[None, :, None],
    ).astype(jnp.bfloat16)
    key_cols = lax.dynamic_slice_in_dim(suffix_keys, kv_head * HD, HD, 2)
    key_rot = rotate(key_cols.astype(jnp.float32), suffix_pos[None, :]).astype(jnp.bfloat16)
    value_cols = lax.dynamic_slice_in_dim(suffix_values, kv_head * HD, HD, 2)
    lengths_all = slot_lengths(suffix_len, slot_request)
    local_len = lax.dynamic_slice_in_dim(lengths_all, req_index * local_slots, local_slots, 0)
    allowed = (places[None, :, None] >= places[None, None, :]) & (
        places[None, None, :] < local_len[:, None, None]
    )
    suffix_scores = (
        jnp.einsum("jthd,jud->jthu", query_rot, key_rot, preferred_element_type=jnp.float32) * scale
    )
    suffix_scores = jnp.where(allowed[:, :, None, :], suffix_scores, MASKED)
    suffix_max = jnp.max(suffix_scores, axis=-1)
    suffix_prob = jnp.exp(suffix_scores - suffix_max[..., None])
    suffix_total = jnp.sum(suffix_prob, axis=-1)
    suffix_acc = jnp.einsum(
        "jthu,jud->jthd",
        suffix_prob.astype(jnp.bfloat16),
        value_cols,
        preferred_element_type=jnp.float32,
    )
    suffix_state = (
        suffix_max.reshape(all_rows),
        suffix_total.reshape(all_rows),
        suffix_acc.reshape(all_rows, HD),
    )
    local_prefix = prefix_cache.shape[0]
    block_count = prefix_block.shape[0]
    row_ids = req_index * local_prefix + jnp.arange(local_prefix, dtype=jnp.int32)
    block_match = (
        (row_ids // PBLK)[:, None] == jnp.arange(block_count, dtype=jnp.int32)[None, :]
    ).astype(jnp.int32)
    logical_block = jnp.sum(block_match * prefix_block[None, :], axis=1)
    pre_pos = (logical_block * PBLK + row_ids % PBLK).astype(jnp.float32)
    pre_keys = rotate(
        lax.dynamic_slice_in_dim(prefix_cache[:, 0], kv_head * HD, HD, 1).astype(jnp.float32),
        pre_pos,
    ).astype(jnp.bfloat16)
    pre_values = lax.dynamic_slice_in_dim(prefix_cache[:, 1], kv_head * HD, HD, 1)
    query_flat = query_rot.reshape(all_rows, HD)
    run_max = jnp.full((all_rows,), MASKED, jnp.float32)
    keys_piece = lax.all_gather(pre_keys, "req", axis=0, tiled=True)
    values_piece = lax.all_gather(pre_values, "req", axis=0, tiled=True)
    scores = (
        jnp.einsum("rd,pd->rp", query_flat, keys_piece, preferred_element_type=jnp.float32) * scale
    )
    new_max = jnp.maximum(run_max, jnp.max(scores, axis=1))
    probs = jnp.exp(scores - new_max[:, None])
    new_total = jnp.sum(probs, axis=1)
    new_acc = jnp.dot(probs.astype(jnp.bfloat16), values_piece, preferred_element_type=jnp.float32)
    final_state = (new_max, new_total, new_acc)
    final_state = merge_states(final_state, suffix_state)
    final_max, final_total, final_acc = final_state
    attn_local = (
        (final_acc / final_total[:, None])
        .astype(jnp.bfloat16)
        .reshape(local_slots * maxlen, head_count * HD)
    )
    tokens = residual.shape[0]
    own_rows = tokens // hid_count
    source = token_source(suffix_len, slot_request, tokens, maxlen)
    token_rows = jnp.take(lax.all_gather(attn_local, "req", axis=0, tiled=True), source, axis=0)
    projected = jnp.dot(token_rows, out_weight, preferred_element_type=jnp.float32)
    summed = exchange_sum(projected.astype(jnp.bfloat16), "hid", hid_count)
    residual_own = lax.dynamic_slice_in_dim(residual, hid_index * own_rows, own_rows, 0)
    resid_own = (residual_own.astype(jnp.float32) + summed).astype(jnp.bfloat16)
    resid_all = exchange_gather(resid_own, "hid", hid_count)
    resid_f = lax.optimization_barrier(resid_all).astype(jnp.float32)
    squares = jnp.sum(resid_f * resid_f, axis=1)
    scaled = (resid_f * post_gain[None, :]).astype(jnp.bfloat16)
    gate_part = jnp.dot(scaled, gate_weight, preferred_element_type=jnp.float32)
    up_part = jnp.dot(scaled, up_weight, preferred_element_type=jnp.float32)
    square_all = lax.psum(squares, "req")
    ff_cols = gate_part.shape[1]
    both_sum = lax.psum_scatter(
        jnp.concatenate([gate_part.astype(jnp.bfloat16), up_part.astype(jnp.bfloat16)], axis=1),
        "req",
        scatter_dimension=0,
        tiled=True,
    ).astype(jnp.float32)
    gate_sum, up_sum = both_sum[:, :ff_cols], both_sum[:, ff_cols:]
    row_count = tokens // req_count
    square_sum = lax.dynamic_slice_in_dim(square_all, req_index * row_count, row_count, 0)
    inv_rms = lax.rsqrt(square_sum / D + EPSILON)
    hidden = (jax.nn.silu(gate_sum * inv_rms[:, None]) * (up_sum * inv_rms[:, None])).astype(
        jnp.bfloat16
    )
    hidden_all = lax.all_gather(hidden, "req", axis=0, tiled=True)
    mixed_rows = exchange_sum(
        jnp.dot(hidden_all, down_weight, preferred_element_type=jnp.float32).astype(jnp.bfloat16),
        "hid",
        hid_count,
    )
    return (resid_own.astype(jnp.float32) + mixed_rows).astype(jnp.bfloat16)


def solution(mesh):
    return jax.shard_map(
        on_device,
        mesh=mesh,
        in_specs=(
            P("req", None, "hid"),
            P("req", None, None),
            P("req", None, None),
            P("req", None, None),
            P(),
            P(),
            P(),
            P(None, "req"),
            P("hid", "req"),
            P("req"),
            P("req", "hid"),
            P("req", "hid"),
            P("hid", "req"),
        ),
        out_specs=P("hid", "req"),
        check_vma=False,
    )
```

```python
import jax
import jax.numpy as jnp
from jax import lax
from jax.experimental import pallas as pl
from jax.experimental.pallas import tpu as pltpu
from jax.sharding import PartitionSpec as P

D = 8192
KVH = 8
HD = 128
PREFIX = 8192
PBLK = 256


ROPE_BASE = 500000.0
EPSILON = 1e-05
MASKED = -1e30


def rotate(vectors, positions):
    half_width = vectors.shape[-1] // 2
    exponent = 2.0 * jnp.arange(half_width, dtype=jnp.float32) / vectors.shape[-1]
    frequency = jnp.exp(-jnp.log(ROPE_BASE) * exponent)
    angles = positions[..., None] * frequency
    cosine = jnp.cos(angles)
    sine_part = jnp.sin(angles)
    lower_half = vectors[..., :half_width]
    upper_half = vectors[..., half_width:]
    return jnp.concatenate(
        [
            lower_half * cosine - upper_half * sine_part,
            upper_half * cosine + lower_half * sine_part,
        ],
        axis=-1,
    )


def slot_lengths(suffix_len, slot_request):
    total_count = suffix_len.shape[0]
    matches = (slot_request[:, None] == jnp.arange(total_count, dtype=jnp.int32)[None, :]).astype(
        jnp.int32
    )
    return jnp.sum(matches * suffix_len[None, :], axis=1)


def token_source(suffix_len, slot_request, tokens, maxlen):
    total_count = suffix_len.shape[0]
    numbers = jnp.arange(total_count, dtype=jnp.int32)
    starts = jnp.cumsum(suffix_len) - suffix_len
    token_ids = jnp.arange(tokens, dtype=jnp.int32)
    reached = (token_ids[:, None] >= starts[None, :]).astype(jnp.int32)
    owner_req = jnp.sum(reached, axis=1) - 1
    onehot = (owner_req[:, None] == numbers[None, :]).astype(jnp.int32)
    start_tok = jnp.sum(onehot * starts[None, :], axis=1)
    inverse = jnp.sum(
        (slot_request[:, None] == numbers[None, :]).astype(jnp.int32) * numbers[:, None], axis=0
    )
    slot_tok = jnp.sum(onehot * inverse[None, :], axis=1)
    return slot_tok * maxlen + token_ids - start_tok


def merge_states(state_one, state_two):
    max_one, total_one, acc_one = state_one
    max_two, total_two, acc_two = state_two
    new_max = jnp.maximum(max_one, max_two)
    shrink_one = jnp.exp(max_one - new_max)
    shrink_two = jnp.exp(max_two - new_max)
    new_total = total_one * shrink_one + total_two * shrink_two
    new_acc = acc_one * shrink_one[:, None] + acc_two * shrink_two[:, None]
    return (new_max, new_total, new_acc)


def exchange_sum(values, axis, count):
    parts = lax.all_to_all(
        values.reshape(count, values.shape[0] // count, values.shape[1]), axis, 0, 0, tiled=True
    )
    return jnp.sum(parts.astype(jnp.float32), axis=0)


def exchange_gather(values, axis, count):
    parts = lax.all_to_all(
        jnp.broadcast_to(values[None], (count,) + values.shape), axis, 0, 0, tiled=True
    )
    return parts.reshape(count * values.shape[0], values.shape[1])


def prefix_kernel(q_ref, k_ref, v_ref, m_ref, l_ref, acc_ref):
    @pl.when(pl.program_id(1) == 0)
    def _():
        m_ref[...] = jnp.full(m_ref.shape, MASKED, jnp.float32)
        l_ref[...] = jnp.zeros(l_ref.shape, jnp.float32)
        acc_ref[...] = jnp.zeros(acc_ref.shape, jnp.float32)

    scores = lax.dot_general(
        q_ref[...], k_ref[...], (((1,), (1,)), ((), ())), preferred_element_type=jnp.float32
    ) * (HD ** (-0.5))
    m_prev = m_ref[...]
    m_new = jnp.maximum(m_prev, jnp.max(scores, axis=1, keepdims=True))
    shrink = jnp.exp(m_prev - m_new)
    probs = jnp.exp(scores - m_new)
    l_ref[...] = shrink * l_ref[...] + jnp.sum(probs, axis=1, keepdims=True)
    acc_ref[...] = shrink * acc_ref[...] + jnp.dot(
        probs.astype(jnp.bfloat16), v_ref[...], preferred_element_type=jnp.float32
    )
    m_ref[...] = m_new


def prefix_attention(query_flat, keys, values, q_tile=512, k_tile=1024):
    rows = query_flat.shape[0]
    length = keys.shape[0]
    return pl.pallas_call(
        prefix_kernel,
        out_shape=(
            jax.ShapeDtypeStruct((rows, 1), jnp.float32),
            jax.ShapeDtypeStruct((rows, 1), jnp.float32),
            jax.ShapeDtypeStruct((rows, HD), jnp.float32),
        ),
        grid=(rows // q_tile, length // k_tile),
        in_specs=[
            pl.BlockSpec((q_tile, HD), lambda i, j: (i, 0)),
            pl.BlockSpec((k_tile, HD), lambda i, j: (j, 0)),
            pl.BlockSpec((k_tile, HD), lambda i, j: (j, 0)),
        ],
        out_specs=(
            pl.BlockSpec((q_tile, 1), lambda i, j: (i, 0)),
            pl.BlockSpec((q_tile, 1), lambda i, j: (i, 0)),
            pl.BlockSpec((q_tile, HD), lambda i, j: (i, 0)),
        ),
        compiler_params=pltpu.CompilerParams(dimension_semantics=("parallel", "arbitrary")),
    )(query_flat, keys, values)


def on_device(
    queries,
    suffix_keys,
    suffix_values,
    prefix_cache,
    prefix_block,
    suffix_len,
    slot_request,
    residual,
    out_weight,
    post_gain,
    gate_weight,
    up_weight,
    down_weight,
):
    hid_count = lax.axis_size("hid")
    req_count = lax.axis_size("req")
    req_index = lax.axis_index("req")
    hid_index = lax.axis_index("hid")
    local_slots, maxlen, query_cols = queries.shape
    head_count = query_cols // HD
    kv_head = hid_index // (hid_count // KVH)
    scale = HD ** (-0.5)
    all_rows = local_slots * maxlen * head_count
    places = jnp.arange(maxlen, dtype=jnp.int32)
    suffix_pos = (PREFIX + places).astype(jnp.float32)
    query_rot = rotate(
        queries.astype(jnp.float32).reshape(local_slots, maxlen, head_count, HD),
        suffix_pos[None, :, None],
    ).astype(jnp.bfloat16)
    key_cols = lax.dynamic_slice_in_dim(suffix_keys, kv_head * HD, HD, 2)
    key_rot = rotate(key_cols.astype(jnp.float32), suffix_pos[None, :]).astype(jnp.bfloat16)
    value_cols = lax.dynamic_slice_in_dim(suffix_values, kv_head * HD, HD, 2)
    lengths_all = slot_lengths(suffix_len, slot_request)
    local_len = lax.dynamic_slice_in_dim(lengths_all, req_index * local_slots, local_slots, 0)
    allowed = (places[None, :, None] >= places[None, None, :]) & (
        places[None, None, :] < local_len[:, None, None]
    )
    suffix_scores = (
        jnp.einsum("jthd,jud->jthu", query_rot, key_rot, preferred_element_type=jnp.float32) * scale
    )
    suffix_scores = jnp.where(allowed[:, :, None, :], suffix_scores, MASKED)
    suffix_max = jnp.max(suffix_scores, axis=-1)
    suffix_prob = jnp.exp(suffix_scores - suffix_max[..., None])
    suffix_total = jnp.sum(suffix_prob, axis=-1)
    suffix_acc = jnp.einsum(
        "jthu,jud->jthd",
        suffix_prob.astype(jnp.bfloat16),
        value_cols,
        preferred_element_type=jnp.float32,
    )
    suffix_state = (
        suffix_max.reshape(all_rows),
        suffix_total.reshape(all_rows),
        suffix_acc.reshape(all_rows, HD),
    )
    local_prefix = prefix_cache.shape[0]
    block_count = prefix_block.shape[0]
    row_ids = req_index * local_prefix + jnp.arange(local_prefix, dtype=jnp.int32)
    block_match = (
        (row_ids // PBLK)[:, None] == jnp.arange(block_count, dtype=jnp.int32)[None, :]
    ).astype(jnp.int32)
    logical_block = jnp.sum(block_match * prefix_block[None, :], axis=1)
    pre_pos = (logical_block * PBLK + row_ids % PBLK).astype(jnp.float32)
    pre_keys = rotate(
        lax.dynamic_slice_in_dim(prefix_cache[:, 0], kv_head * HD, HD, 1).astype(jnp.float32),
        pre_pos,
    ).astype(jnp.bfloat16)
    pre_values = lax.dynamic_slice_in_dim(prefix_cache[:, 1], kv_head * HD, HD, 1)
    query_flat = query_rot.reshape(all_rows, HD)
    keys_piece = lax.all_gather(pre_keys, "req", axis=0, tiled=True)
    values_piece = lax.all_gather(pre_values, "req", axis=0, tiled=True)
    new_max, new_total, new_acc = prefix_attention(query_flat, keys_piece, values_piece)
    final_state = (new_max.reshape(all_rows), new_total.reshape(all_rows), new_acc)
    final_state = merge_states(final_state, suffix_state)
    final_max, final_total, final_acc = final_state
    attn_local = (
        (final_acc / final_total[:, None])
        .astype(jnp.bfloat16)
        .reshape(local_slots * maxlen, head_count * HD)
    )
    tokens = residual.shape[0]
    own_rows = tokens // hid_count
    source = token_source(suffix_len, slot_request, tokens, maxlen)
    token_rows = jnp.take(lax.all_gather(attn_local, "req", axis=0, tiled=True), source, axis=0)
    projected = jnp.dot(token_rows, out_weight, preferred_element_type=jnp.float32)
    summed = exchange_sum(projected.astype(jnp.bfloat16), "hid", hid_count)
    residual_own = lax.dynamic_slice_in_dim(residual, hid_index * own_rows, own_rows, 0)
    resid_own = (residual_own.astype(jnp.float32) + summed).astype(jnp.bfloat16)
    resid_all = exchange_gather(resid_own, "hid", hid_count)
    resid_f = lax.optimization_barrier(resid_all).astype(jnp.float32)
    squares = jnp.sum(resid_f * resid_f, axis=1)
    scaled = (resid_f * post_gain[None, :]).astype(jnp.bfloat16)
    gate_part = jnp.dot(scaled, gate_weight, preferred_element_type=jnp.float32)
    up_part = jnp.dot(scaled, up_weight, preferred_element_type=jnp.float32)
    square_all = lax.psum(squares, "req")
    ff_cols = gate_part.shape[1]
    both_sum = lax.psum_scatter(
        jnp.concatenate([gate_part.astype(jnp.bfloat16), up_part.astype(jnp.bfloat16)], axis=1),
        "req",
        scatter_dimension=0,
        tiled=True,
    ).astype(jnp.float32)
    gate_sum, up_sum = both_sum[:, :ff_cols], both_sum[:, ff_cols:]
    row_count = tokens // req_count
    square_sum = lax.dynamic_slice_in_dim(square_all, req_index * row_count, row_count, 0)
    inv_rms = lax.rsqrt(square_sum / D + EPSILON)
    hidden = (jax.nn.silu(gate_sum * inv_rms[:, None]) * (up_sum * inv_rms[:, None])).astype(
        jnp.bfloat16
    )
    hidden_all = lax.all_gather(hidden, "req", axis=0, tiled=True)
    mixed_rows = exchange_sum(
        jnp.dot(hidden_all, down_weight, preferred_element_type=jnp.float32).astype(jnp.bfloat16),
        "hid",
        hid_count,
    )
    return (resid_own.astype(jnp.float32) + mixed_rows).astype(jnp.bfloat16)


def solution(mesh):
    return jax.shard_map(
        on_device,
        mesh=mesh,
        in_specs=(
            P("req", None, "hid"),
            P("req", None, None),
            P("req", None, None),
            P("req", None, None),
            P(),
            P(),
            P(),
            P(None, "req"),
            P("hid", "req"),
            P("req"),
            P("req", "hid"),
            P("req", "hid"),
            P("hid", "req"),
        ),
        out_specs=P("hid", "req"),
        check_vma=False,
    )
```

```python
import jax
import jax.numpy as jnp
from jax import lax
from jax.sharding import PartitionSpec as P

D = 8192
KVH = 8
HD = 128
PREFIX = 8192
PBLK = 256


ROPE_BASE = 500000.0
EPSILON = 1e-05
MASKED = -1e30


def rotate(vectors, positions):
    half_width = vectors.shape[-1] // 2
    exponent = 2.0 * jnp.arange(half_width, dtype=jnp.float32) / vectors.shape[-1]
    frequency = jnp.exp(-jnp.log(ROPE_BASE) * exponent)
    angles = positions[..., None] * frequency
    cosine = jnp.cos(angles)
    sine_part = jnp.sin(angles)
    lower_half = vectors[..., :half_width]
    upper_half = vectors[..., half_width:]
    return jnp.concatenate(
        [
            lower_half * cosine - upper_half * sine_part,
            upper_half * cosine + lower_half * sine_part,
        ],
        axis=-1,
    )


def slot_lengths(suffix_len, slot_request):
    total_count = suffix_len.shape[0]
    matches = (slot_request[:, None] == jnp.arange(total_count, dtype=jnp.int32)[None, :]).astype(
        jnp.int32
    )
    return jnp.sum(matches * suffix_len[None, :], axis=1)


def token_source(suffix_len, slot_request, tokens, maxlen):
    total_count = suffix_len.shape[0]
    numbers = jnp.arange(total_count, dtype=jnp.int32)
    starts = jnp.cumsum(suffix_len) - suffix_len
    token_ids = jnp.arange(tokens, dtype=jnp.int32)
    reached = (token_ids[:, None] >= starts[None, :]).astype(jnp.int32)
    owner_req = jnp.sum(reached, axis=1) - 1
    onehot = (owner_req[:, None] == numbers[None, :]).astype(jnp.int32)
    start_tok = jnp.sum(onehot * starts[None, :], axis=1)
    inverse = jnp.sum(
        (slot_request[:, None] == numbers[None, :]).astype(jnp.int32) * numbers[:, None], axis=0
    )
    slot_tok = jnp.sum(onehot * inverse[None, :], axis=1)
    return slot_tok * maxlen + token_ids - start_tok


def merge_states(state_one, state_two):
    max_one, total_one, acc_one = state_one
    max_two, total_two, acc_two = state_two
    new_max = jnp.maximum(max_one, max_two)
    shrink_one = jnp.exp(max_one - new_max)
    shrink_two = jnp.exp(max_two - new_max)
    new_total = total_one * shrink_one + total_two * shrink_two
    new_acc = acc_one * shrink_one[:, None] + acc_two * shrink_two[:, None]
    return (new_max, new_total, new_acc)


def exchange_sum(values, axis, count):
    parts = lax.all_to_all(
        values.reshape(count, values.shape[0] // count, values.shape[1]), axis, 0, 0, tiled=True
    )
    return jnp.sum(parts.astype(jnp.float32), axis=0)


def exchange_gather(values, axis, count):
    parts = lax.all_to_all(
        jnp.broadcast_to(values[None], (count,) + values.shape), axis, 0, 0, tiled=True
    )
    return parts.reshape(count * values.shape[0], values.shape[1])


def on_device(
    queries,
    suffix_keys,
    suffix_values,
    prefix_cache,
    prefix_block,
    suffix_len,
    slot_request,
    residual,
    out_weight,
    post_gain,
    gate_weight,
    up_weight,
    down_weight,
):
    hid_count = lax.axis_size("hid")
    req_count = lax.axis_size("req")
    req_index = lax.axis_index("req")
    hid_index = lax.axis_index("hid")
    local_slots, maxlen, query_cols = queries.shape
    head_count = query_cols // HD
    kv_head = hid_index // (hid_count // KVH)
    scale = HD ** (-0.5)
    all_rows = local_slots * maxlen * head_count
    places = jnp.arange(maxlen, dtype=jnp.int32)
    suffix_pos = (PREFIX + places).astype(jnp.float32)
    query_rot = rotate(
        queries.astype(jnp.float32).reshape(local_slots, maxlen, head_count, HD),
        suffix_pos[None, :, None],
    ).astype(jnp.bfloat16)
    key_cols = lax.dynamic_slice_in_dim(suffix_keys, kv_head * HD, HD, 2)
    key_rot = rotate(key_cols.astype(jnp.float32), suffix_pos[None, :]).astype(jnp.bfloat16)
    value_cols = lax.dynamic_slice_in_dim(suffix_values, kv_head * HD, HD, 2)
    lengths_all = slot_lengths(suffix_len, slot_request)
    local_len = lax.dynamic_slice_in_dim(lengths_all, req_index * local_slots, local_slots, 0)
    allowed = (places[None, :, None] >= places[None, None, :]) & (
        places[None, None, :] < local_len[:, None, None]
    )
    suffix_scores = (
        jnp.einsum("jthd,jud->jthu", query_rot, key_rot, preferred_element_type=jnp.float32) * scale
    )
    suffix_scores = jnp.where(allowed[:, :, None, :], suffix_scores, MASKED)
    suffix_max = jnp.max(suffix_scores, axis=-1)
    suffix_prob = jnp.exp(suffix_scores - suffix_max[..., None])
    suffix_total = jnp.sum(suffix_prob, axis=-1)
    suffix_acc = jnp.einsum(
        "jthu,jud->jthd",
        suffix_prob.astype(jnp.bfloat16),
        value_cols,
        preferred_element_type=jnp.float32,
    )
    suffix_state = (
        suffix_max.reshape(all_rows),
        suffix_total.reshape(all_rows),
        suffix_acc.reshape(all_rows, HD),
    )
    local_prefix = prefix_cache.shape[0]
    block_count = prefix_block.shape[0]
    row_ids = req_index * local_prefix + jnp.arange(local_prefix, dtype=jnp.int32)
    block_match = (
        (row_ids // PBLK)[:, None] == jnp.arange(block_count, dtype=jnp.int32)[None, :]
    ).astype(jnp.int32)
    logical_block = jnp.sum(block_match * prefix_block[None, :], axis=1)
    pre_pos = (logical_block * PBLK + row_ids % PBLK).astype(jnp.float32)
    key_block = lax.dynamic_slice(prefix_cache, (0, 0, kv_head * HD), (local_prefix, 1, HD))
    pre_keys = rotate(key_block.reshape(local_prefix, HD).astype(jnp.float32), pre_pos).astype(
        jnp.bfloat16
    )
    value_block = lax.dynamic_slice(prefix_cache, (0, 1, kv_head * HD), (local_prefix, 1, HD))
    pre_values = value_block.reshape(local_prefix, HD)
    query_flat = query_rot.reshape(all_rows, HD)
    run_max = jnp.full((all_rows,), MASKED, jnp.float32)
    keys_piece = lax.all_gather(pre_keys, "req", axis=0, tiled=True)
    values_piece = lax.all_gather(pre_values, "req", axis=0, tiled=True)
    scores = (
        jnp.einsum("rd,pd->rp", query_flat, keys_piece, preferred_element_type=jnp.float32) * scale
    )
    new_max = jnp.maximum(run_max, jnp.max(scores, axis=1))
    probs = jnp.exp(scores - new_max[:, None])
    new_total = jnp.sum(probs, axis=1)
    new_acc = jnp.dot(probs.astype(jnp.bfloat16), values_piece, preferred_element_type=jnp.float32)
    final_state = (new_max, new_total, new_acc)
    final_state = merge_states(final_state, suffix_state)
    final_max, final_total, final_acc = final_state
    attn_local = (
        (final_acc / final_total[:, None])
        .astype(jnp.bfloat16)
        .reshape(local_slots * maxlen, head_count * HD)
    )
    tokens = residual.shape[0]
    own_rows = tokens // hid_count
    source = token_source(suffix_len, slot_request, tokens, maxlen)
    token_rows = jnp.take(lax.all_gather(attn_local, "req", axis=0, tiled=True), source, axis=0)
    projected = jnp.dot(token_rows, out_weight, preferred_element_type=jnp.float32)
    summed = exchange_sum(projected.astype(jnp.bfloat16), "hid", hid_count)
    residual_own = lax.dynamic_slice_in_dim(residual, hid_index * own_rows, own_rows, 0)
    resid_own = (residual_own.astype(jnp.float32) + summed).astype(jnp.bfloat16)
    resid_all = exchange_gather(resid_own, "hid", hid_count)
    resid_f = lax.optimization_barrier(resid_all).astype(jnp.float32)
    squares = jnp.sum(resid_f * resid_f, axis=1)
    scaled = (resid_f * post_gain[None, :]).astype(jnp.bfloat16)
    gate_part = jnp.dot(scaled, gate_weight, preferred_element_type=jnp.float32)
    up_part = jnp.dot(scaled, up_weight, preferred_element_type=jnp.float32)
    square_all = lax.psum(squares, "req")
    ff_cols = gate_part.shape[1]
    both_sum = lax.psum_scatter(
        jnp.concatenate([gate_part.astype(jnp.bfloat16), up_part.astype(jnp.bfloat16)], axis=1),
        "req",
        scatter_dimension=0,
        tiled=True,
    ).astype(jnp.float32)
    gate_sum, up_sum = both_sum[:, :ff_cols], both_sum[:, ff_cols:]
    row_count = tokens // req_count
    square_sum = lax.dynamic_slice_in_dim(square_all, req_index * row_count, row_count, 0)
    inv_rms = lax.rsqrt(square_sum / D + EPSILON)
    hidden = (jax.nn.silu(gate_sum * inv_rms[:, None]) * (up_sum * inv_rms[:, None])).astype(
        jnp.bfloat16
    )
    hidden_all = lax.all_gather(hidden, "req", axis=0, tiled=True)
    mixed_rows = exchange_sum(
        jnp.dot(hidden_all, down_weight, preferred_element_type=jnp.float32).astype(jnp.bfloat16),
        "hid",
        hid_count,
    )
    return (resid_own.astype(jnp.float32) + mixed_rows).astype(jnp.bfloat16)


def solution(mesh):
    return jax.shard_map(
        on_device,
        mesh=mesh,
        in_specs=(
            P("req", None, "hid"),
            P("req", None, None),
            P("req", None, None),
            P("req", None, None),
            P(),
            P(),
            P(),
            P(None, "req"),
            P("hid", "req"),
            P("req"),
            P("req", "hid"),
            P("req", "hid"),
            P("hid", "req"),
        ),
        out_specs=P("hid", "req"),
        check_vma=False,
    )
```

```python
import jax
import jax.numpy as jnp
from jax import lax
from jax.sharding import PartitionSpec as P

D = 8192
KVH = 8
HD = 128
PREFIX = 8192
PBLK = 256


ROPE_BASE = 500000.0
EPSILON = 1e-05
MASKED = -1e30


def rotate(vectors, positions):
    half_width = vectors.shape[-1] // 2
    exponent = 2.0 * jnp.arange(half_width, dtype=jnp.float32) / vectors.shape[-1]
    frequency = jnp.exp(-jnp.log(ROPE_BASE) * exponent)
    angles = positions[..., None] * frequency
    cosine = jnp.cos(angles)
    sine_part = jnp.sin(angles)
    lower_half = vectors[..., :half_width]
    upper_half = vectors[..., half_width:]
    return jnp.concatenate(
        [
            lower_half * cosine - upper_half * sine_part,
            upper_half * cosine + lower_half * sine_part,
        ],
        axis=-1,
    )


def slot_lengths(suffix_len, slot_request):
    total_count = suffix_len.shape[0]
    matches = (slot_request[:, None] == jnp.arange(total_count, dtype=jnp.int32)[None, :]).astype(
        jnp.int32
    )
    return jnp.sum(matches * suffix_len[None, :], axis=1)


def token_source(suffix_len, slot_request, tokens, maxlen):
    total_count = suffix_len.shape[0]
    numbers = jnp.arange(total_count, dtype=jnp.int32)
    starts = jnp.cumsum(suffix_len) - suffix_len
    token_ids = jnp.arange(tokens, dtype=jnp.int32)
    reached = (token_ids[:, None] >= starts[None, :]).astype(jnp.int32)
    owner_req = jnp.sum(reached, axis=1) - 1
    onehot = (owner_req[:, None] == numbers[None, :]).astype(jnp.int32)
    start_tok = jnp.sum(onehot * starts[None, :], axis=1)
    inverse = jnp.sum(
        (slot_request[:, None] == numbers[None, :]).astype(jnp.int32) * numbers[:, None], axis=0
    )
    slot_tok = jnp.sum(onehot * inverse[None, :], axis=1)
    return slot_tok * maxlen + token_ids - start_tok


def merge_states(state_one, state_two):
    max_one, total_one, acc_one = state_one
    max_two, total_two, acc_two = state_two
    new_max = jnp.maximum(max_one, max_two)
    shrink_one = jnp.exp(max_one - new_max)
    shrink_two = jnp.exp(max_two - new_max)
    new_total = total_one * shrink_one + total_two * shrink_two
    new_acc = acc_one * shrink_one[:, None] + acc_two * shrink_two[:, None]
    return (new_max, new_total, new_acc)


def exchange_sum(values, axis, count):
    parts = lax.all_to_all(
        values.reshape(count, values.shape[0] // count, values.shape[1]), axis, 0, 0, tiled=True
    )
    return jnp.sum(parts.astype(jnp.float32), axis=0)


def exchange_gather(values, axis, count):
    parts = lax.all_to_all(
        jnp.broadcast_to(values[None], (count,) + values.shape), axis, 0, 0, tiled=True
    )
    return parts.reshape(count * values.shape[0], values.shape[1])


def on_device(
    queries,
    suffix_keys,
    suffix_values,
    prefix_cache,
    prefix_block,
    suffix_len,
    slot_request,
    residual,
    out_weight,
    post_gain,
    gate_weight,
    up_weight,
    down_weight,
):
    hid_count = lax.axis_size("hid")
    req_count = lax.axis_size("req")
    req_index = lax.axis_index("req")
    hid_index = lax.axis_index("hid")
    local_slots, maxlen, query_cols = queries.shape
    head_count = query_cols // HD
    kv_head = hid_index // (hid_count // KVH)
    scale = HD ** (-0.5)
    all_rows = local_slots * maxlen * head_count
    places = jnp.arange(maxlen, dtype=jnp.int32)
    suffix_pos = (PREFIX + places).astype(jnp.float32)
    query_rot = rotate(
        queries.astype(jnp.float32).reshape(local_slots, maxlen, head_count, HD),
        suffix_pos[None, :, None],
    ).astype(jnp.bfloat16)
    key_cols = lax.dynamic_slice_in_dim(suffix_keys, kv_head * HD, HD, 2)
    key_rot = rotate(key_cols.astype(jnp.float32), suffix_pos[None, :]).astype(jnp.bfloat16)
    value_cols = lax.dynamic_slice_in_dim(suffix_values, kv_head * HD, HD, 2)
    lengths_all = slot_lengths(suffix_len, slot_request)
    local_len = lax.dynamic_slice_in_dim(lengths_all, req_index * local_slots, local_slots, 0)
    allowed = (places[None, :, None] >= places[None, None, :]) & (
        places[None, None, :] < local_len[:, None, None]
    )
    suffix_scores = (
        jnp.einsum("jthd,jud->jthu", query_rot, key_rot, preferred_element_type=jnp.float32) * scale
    )
    suffix_scores = jnp.where(allowed[:, :, None, :], suffix_scores, MASKED)
    suffix_max = jnp.max(suffix_scores, axis=-1)
    suffix_prob = jnp.exp(suffix_scores - suffix_max[..., None])
    suffix_total = jnp.sum(suffix_prob, axis=-1)
    suffix_acc = jnp.einsum(
        "jthu,jud->jthd",
        suffix_prob.astype(jnp.bfloat16),
        value_cols,
        preferred_element_type=jnp.float32,
    )
    suffix_state = (
        suffix_max.reshape(all_rows),
        suffix_total.reshape(all_rows),
        suffix_acc.reshape(all_rows, HD),
    )
    local_prefix = prefix_cache.shape[0]
    block_count = prefix_block.shape[0]
    row_ids = req_index * local_prefix + jnp.arange(local_prefix, dtype=jnp.int32)
    block_match = (
        (row_ids // PBLK)[:, None] == jnp.arange(block_count, dtype=jnp.int32)[None, :]
    ).astype(jnp.int32)
    logical_block = jnp.sum(block_match * prefix_block[None, :], axis=1)
    pre_pos = (logical_block * PBLK + row_ids % PBLK).astype(jnp.float32)
    key_block = lax.dynamic_slice(prefix_cache, (0, 0, kv_head * HD), (local_prefix, 1, HD))
    pre_keys = rotate(key_block.reshape(local_prefix, HD).astype(jnp.float32), pre_pos).astype(
        jnp.bfloat16
    )
    value_block = lax.dynamic_slice(prefix_cache, (0, 1, kv_head * HD), (local_prefix, 1, HD))
    pre_values = value_block.reshape(local_prefix, HD)
    query_flat = query_rot.reshape(all_rows, HD)
    run_max = jnp.full((all_rows,), MASKED, jnp.float32)
    keys_piece = lax.all_gather(pre_keys, "req", axis=0, tiled=True)
    values_piece = lax.all_gather(pre_values, "req", axis=0, tiled=True)
    scores = (
        jnp.einsum("rd,pd->rp", query_flat, keys_piece, preferred_element_type=jnp.float32) * scale
    )
    new_max = jnp.maximum(run_max, jnp.max(scores, axis=1))
    probs = jnp.exp(scores - new_max[:, None])
    new_total = jnp.sum(probs, axis=1)
    new_acc = jnp.dot(probs.astype(jnp.bfloat16), values_piece, preferred_element_type=jnp.float32)
    final_state = (new_max, new_total, new_acc)
    final_state = merge_states(final_state, suffix_state)
    final_max, final_total, final_acc = final_state
    attn_local = (
        (final_acc / final_total[:, None])
        .astype(jnp.bfloat16)
        .reshape(local_slots * maxlen, head_count * HD)
    )
    tokens = residual.shape[0]
    own_rows = tokens // hid_count
    source = token_source(suffix_len, slot_request, tokens, maxlen)
    token_rows = jnp.take(lax.all_gather(attn_local, "req", axis=0, tiled=True), source, axis=0)
    projected = jnp.dot(token_rows, out_weight, preferred_element_type=jnp.float32).astype(
        jnp.bfloat16
    )
    halves = 2
    half = tokens // halves
    piece = half // hid_count
    row_count = half // req_count
    ff_cols = gate_weight.shape[1]
    resid_halves, square_halves, both_halves = [], [], []
    for c in range(halves):
        summed = exchange_sum(projected[c * half : (c + 1) * half], "hid", hid_count)
        residual_piece = lax.dynamic_slice_in_dim(residual, c * half + hid_index * piece, piece, 0)
        resid_piece = (residual_piece.astype(jnp.float32) + summed).astype(jnp.bfloat16)
        resid_half = exchange_gather(resid_piece, "hid", hid_count)
        resid_halves.append(resid_half)
        resid_f = lax.optimization_barrier(resid_half).astype(jnp.float32)
        square_halves.append(jnp.sum(resid_f * resid_f, axis=1))
        scaled = (resid_f * post_gain[None, :]).astype(jnp.bfloat16)
        gate_part = jnp.dot(scaled, gate_weight, preferred_element_type=jnp.float32)
        up_part = jnp.dot(scaled, up_weight, preferred_element_type=jnp.float32)
        both_halves.append(
            lax.psum_scatter(
                jnp.concatenate(
                    [gate_part.astype(jnp.bfloat16), up_part.astype(jnp.bfloat16)], axis=1
                ),
                "req",
                scatter_dimension=0,
                tiled=True,
            ).astype(jnp.float32)
        )
    square_all = lax.psum(jnp.concatenate(square_halves), "req")
    hidden_halves = []
    for c in range(halves):
        square_sum = lax.dynamic_slice_in_dim(
            square_all, c * half + req_index * row_count, row_count, 0
        )
        inv_rms = lax.rsqrt(square_sum / D + EPSILON)
        gate_sum, up_sum = both_halves[c][:, :ff_cols], both_halves[c][:, ff_cols:]
        hidden_halves.append(
            (jax.nn.silu(gate_sum * inv_rms[:, None]) * (up_sum * inv_rms[:, None])).astype(
                jnp.bfloat16
            )
        )
    hidden_all = lax.all_gather(jnp.concatenate(hidden_halves), "req", axis=0, tiled=True)
    down = jnp.dot(hidden_all, down_weight, preferred_element_type=jnp.float32).astype(
        jnp.bfloat16
    )
    width = down.shape[1]
    down = (
        down.reshape(req_count, halves, row_count, width)
        .transpose(1, 0, 2, 3)
        .reshape(tokens, width)
    )
    mixed_rows = exchange_sum(down, "hid", hid_count)
    resid_own = lax.dynamic_slice_in_dim(
        jnp.concatenate(resid_halves), hid_index * own_rows, own_rows, 0
    )
    return (resid_own.astype(jnp.float32) + mixed_rows).astype(jnp.bfloat16)


def solution(mesh):
    return jax.shard_map(
        on_device,
        mesh=mesh,
        in_specs=(
            P("req", None, "hid"),
            P("req", None, None),
            P("req", None, None),
            P("req", None, None),
            P(),
            P(),
            P(),
            P(None, "req"),
            P("hid", "req"),
            P("req"),
            P("req", "hid"),
            P("req", "hid"),
            P("hid", "req"),
        ),
        out_specs=P("hid", "req"),
        check_vma=False,
    )
```

```python
import jax
import jax.numpy as jnp
from jax import lax
from jax.experimental import pallas as pl
from jax.experimental.pallas import tpu as pltpu
from jax.sharding import PartitionSpec as P

D = 8192
KVH = 8
HD = 128
PREFIX = 8192
PBLK = 256


ROPE_BASE = 500000.0
EPSILON = 1e-05
MASKED = -1e30


def rotate(vectors, positions):
    half_width = vectors.shape[-1] // 2
    exponent = 2.0 * jnp.arange(half_width, dtype=jnp.float32) / vectors.shape[-1]
    frequency = jnp.exp(-jnp.log(ROPE_BASE) * exponent)
    angles = positions[..., None] * frequency
    cosine = jnp.cos(angles)
    sine_part = jnp.sin(angles)
    lower_half = vectors[..., :half_width]
    upper_half = vectors[..., half_width:]
    return jnp.concatenate(
        [
            lower_half * cosine - upper_half * sine_part,
            upper_half * cosine + lower_half * sine_part,
        ],
        axis=-1,
    )


def slot_lengths(suffix_len, slot_request):
    total_count = suffix_len.shape[0]
    matches = (slot_request[:, None] == jnp.arange(total_count, dtype=jnp.int32)[None, :]).astype(
        jnp.int32
    )
    return jnp.sum(matches * suffix_len[None, :], axis=1)


def token_source(suffix_len, slot_request, tokens, maxlen):
    total_count = suffix_len.shape[0]
    numbers = jnp.arange(total_count, dtype=jnp.int32)
    starts = jnp.cumsum(suffix_len) - suffix_len
    token_ids = jnp.arange(tokens, dtype=jnp.int32)
    reached = (token_ids[:, None] >= starts[None, :]).astype(jnp.int32)
    owner_req = jnp.sum(reached, axis=1) - 1
    onehot = (owner_req[:, None] == numbers[None, :]).astype(jnp.int32)
    start_tok = jnp.sum(onehot * starts[None, :], axis=1)
    inverse = jnp.sum(
        (slot_request[:, None] == numbers[None, :]).astype(jnp.int32) * numbers[:, None], axis=0
    )
    slot_tok = jnp.sum(onehot * inverse[None, :], axis=1)
    return slot_tok * maxlen + token_ids - start_tok


def merge_states(state_one, state_two):
    max_one, total_one, acc_one = state_one
    max_two, total_two, acc_two = state_two
    new_max = jnp.maximum(max_one, max_two)
    shrink_one = jnp.exp(max_one - new_max)
    shrink_two = jnp.exp(max_two - new_max)
    new_total = total_one * shrink_one + total_two * shrink_two
    new_acc = acc_one * shrink_one[:, None] + acc_two * shrink_two[:, None]
    return (new_max, new_total, new_acc)


def exchange_sum(values, axis, count):
    parts = lax.all_to_all(
        values.reshape(count, values.shape[0] // count, values.shape[1]), axis, 0, 0, tiled=True
    )
    return jnp.sum(parts.astype(jnp.float32), axis=0)


def exchange_gather(values, axis, count):
    parts = lax.all_to_all(
        jnp.broadcast_to(values[None], (count,) + values.shape), axis, 0, 0, tiled=True
    )
    return parts.reshape(count * values.shape[0], values.shape[1])


def prefix_kernel(q_ref, k_ref, v_ref, m_ref, l_ref, acc_ref):
    @pl.when(pl.program_id(1) == 0)
    def _():
        m_ref[...] = jnp.full(m_ref.shape, MASKED, jnp.float32)
        l_ref[...] = jnp.zeros(l_ref.shape, jnp.float32)
        acc_ref[...] = jnp.zeros(acc_ref.shape, jnp.float32)

    scores = lax.dot_general(
        q_ref[...], k_ref[...], (((1,), (1,)), ((), ())), preferred_element_type=jnp.float32
    ) * (HD ** (-0.5))
    m_prev = m_ref[...]
    m_new = jnp.maximum(m_prev, jnp.max(scores, axis=1, keepdims=True))
    shrink = jnp.exp(m_prev - m_new)
    probs = jnp.exp(scores - m_new)
    l_ref[...] = shrink * l_ref[...] + jnp.sum(probs, axis=1, keepdims=True)
    acc_ref[...] = shrink * acc_ref[...] + jnp.dot(
        probs.astype(jnp.bfloat16), v_ref[...], preferred_element_type=jnp.float32
    )
    m_ref[...] = m_new


def prefix_attention(query_flat, keys_values, q_tile=512, k_tile=1024):
    rows = query_flat.shape[0]
    length = keys_values.shape[0]
    return pl.pallas_call(
        prefix_kernel,
        out_shape=(
            jax.ShapeDtypeStruct((rows, 1), jnp.float32),
            jax.ShapeDtypeStruct((rows, 1), jnp.float32),
            jax.ShapeDtypeStruct((rows, HD), jnp.float32),
        ),
        grid=(rows // q_tile, length // k_tile),
        in_specs=[
            pl.BlockSpec((q_tile, HD), lambda i, j: (i, 0)),
            pl.BlockSpec((k_tile, HD), lambda i, j: (j, 0)),
            pl.BlockSpec((k_tile, HD), lambda i, j: (j, 1)),
        ],
        out_specs=(
            pl.BlockSpec((q_tile, 1), lambda i, j: (i, 0)),
            pl.BlockSpec((q_tile, 1), lambda i, j: (i, 0)),
            pl.BlockSpec((q_tile, HD), lambda i, j: (i, 0)),
        ),
        compiler_params=pltpu.CompilerParams(dimension_semantics=("parallel", "arbitrary")),
    )(query_flat, keys_values, keys_values)


def on_device(
    queries,
    suffix_keys,
    suffix_values,
    prefix_cache,
    prefix_block,
    suffix_len,
    slot_request,
    residual,
    out_weight,
    post_gain,
    gate_weight,
    up_weight,
    down_weight,
):
    hid_count = lax.axis_size("hid")
    req_count = lax.axis_size("req")
    req_index = lax.axis_index("req")
    hid_index = lax.axis_index("hid")
    local_slots, maxlen, query_cols = queries.shape
    head_count = query_cols // HD
    kv_head = hid_index // (hid_count // KVH)
    scale = HD ** (-0.5)
    all_rows = local_slots * maxlen * head_count
    places = jnp.arange(maxlen, dtype=jnp.int32)
    suffix_pos = (PREFIX + places).astype(jnp.float32)
    query_rot = rotate(
        queries.astype(jnp.float32).reshape(local_slots, maxlen, head_count, HD),
        suffix_pos[None, :, None],
    ).astype(jnp.bfloat16)
    key_cols = lax.dynamic_slice_in_dim(suffix_keys, kv_head * HD, HD, 2)
    key_rot = rotate(key_cols.astype(jnp.float32), suffix_pos[None, :]).astype(jnp.bfloat16)
    value_cols = lax.dynamic_slice_in_dim(suffix_values, kv_head * HD, HD, 2)
    lengths_all = slot_lengths(suffix_len, slot_request)
    local_len = lax.dynamic_slice_in_dim(lengths_all, req_index * local_slots, local_slots, 0)
    allowed = (places[None, :, None] >= places[None, None, :]) & (
        places[None, None, :] < local_len[:, None, None]
    )
    suffix_scores = (
        jnp.einsum("jthd,jud->jthu", query_rot, key_rot, preferred_element_type=jnp.float32) * scale
    )
    suffix_scores = jnp.where(allowed[:, :, None, :], suffix_scores, MASKED)
    suffix_max = jnp.max(suffix_scores, axis=-1)
    suffix_prob = jnp.exp(suffix_scores - suffix_max[..., None])
    suffix_total = jnp.sum(suffix_prob, axis=-1)
    suffix_acc = jnp.einsum(
        "jthu,jud->jthd",
        suffix_prob.astype(jnp.bfloat16),
        value_cols,
        preferred_element_type=jnp.float32,
    )
    suffix_state = (
        suffix_max.reshape(all_rows),
        suffix_total.reshape(all_rows),
        suffix_acc.reshape(all_rows, HD),
    )
    local_prefix = prefix_cache.shape[0]
    block_count = prefix_block.shape[0]
    row_ids = req_index * local_prefix + jnp.arange(local_prefix, dtype=jnp.int32)
    block_match = (
        (row_ids // PBLK)[:, None] == jnp.arange(block_count, dtype=jnp.int32)[None, :]
    ).astype(jnp.int32)
    logical_block = jnp.sum(block_match * prefix_block[None, :], axis=1)
    pre_pos = (logical_block * PBLK + row_ids % PBLK).astype(jnp.float32)
    key_block = lax.dynamic_slice(prefix_cache, (0, 0, kv_head * HD), (local_prefix, 1, HD))
    pre_keys = rotate(key_block.reshape(local_prefix, HD).astype(jnp.float32), pre_pos).astype(
        jnp.bfloat16
    )
    value_block = lax.dynamic_slice(prefix_cache, (0, 1, kv_head * HD), (local_prefix, 1, HD))
    pre_values = value_block.reshape(local_prefix, HD)
    query_flat = query_rot.reshape(all_rows, HD)
    keys_values = lax.all_gather(
        jnp.concatenate([pre_keys, pre_values], axis=1), "req", axis=0, tiled=True
    )
    new_max, new_total, new_acc = prefix_attention(query_flat, keys_values)
    final_state = (new_max.reshape(all_rows), new_total.reshape(all_rows), new_acc)
    final_state = merge_states(final_state, suffix_state)
    final_max, final_total, final_acc = final_state
    attn_local = (
        (final_acc / final_total[:, None])
        .astype(jnp.bfloat16)
        .reshape(local_slots * maxlen, head_count * HD)
    )
    tokens = residual.shape[0]
    own_rows = tokens // hid_count
    source = token_source(suffix_len, slot_request, tokens, maxlen)
    token_rows = jnp.take(lax.all_gather(attn_local, "req", axis=0, tiled=True), source, axis=0)
    projected = jnp.dot(token_rows, out_weight, preferred_element_type=jnp.float32)
    summed = exchange_sum(projected.astype(jnp.bfloat16), "hid", hid_count)
    residual_own = lax.dynamic_slice_in_dim(residual, hid_index * own_rows, own_rows, 0)
    resid_own = (residual_own.astype(jnp.float32) + summed).astype(jnp.bfloat16)
    resid_all = exchange_gather(resid_own, "hid", hid_count)
    resid_f = lax.optimization_barrier(resid_all).astype(jnp.float32)
    squares = jnp.sum(resid_f * resid_f, axis=1)
    scaled = (resid_f * post_gain[None, :]).astype(jnp.bfloat16)
    gate_part = jnp.dot(scaled, gate_weight, preferred_element_type=jnp.float32)
    up_part = jnp.dot(scaled, up_weight, preferred_element_type=jnp.float32)
    square_all = lax.psum(squares, "req")
    ff_cols = gate_part.shape[1]
    both_sum = lax.psum_scatter(
        jnp.concatenate([gate_part.astype(jnp.bfloat16), up_part.astype(jnp.bfloat16)], axis=1),
        "req",
        scatter_dimension=0,
        tiled=True,
    ).astype(jnp.float32)
    gate_sum, up_sum = both_sum[:, :ff_cols], both_sum[:, ff_cols:]
    row_count = tokens // req_count
    square_sum = lax.dynamic_slice_in_dim(square_all, req_index * row_count, row_count, 0)
    inv_rms = lax.rsqrt(square_sum / D + EPSILON)
    hidden = (jax.nn.silu(gate_sum * inv_rms[:, None]) * (up_sum * inv_rms[:, None])).astype(
        jnp.bfloat16
    )
    hidden_all = lax.all_gather(hidden, "req", axis=0, tiled=True)
    mixed_rows = exchange_sum(
        jnp.dot(hidden_all, down_weight, preferred_element_type=jnp.float32).astype(jnp.bfloat16),
        "hid",
        hid_count,
    )
    return (resid_own.astype(jnp.float32) + mixed_rows).astype(jnp.bfloat16)


def solution(mesh):
    return jax.shard_map(
        on_device,
        mesh=mesh,
        in_specs=(
            P("req", None, "hid"),
            P("req", None, None),
            P("req", None, None),
            P("req", None, None),
            P(),
            P(),
            P(),
            P(None, "req"),
            P("hid", "req"),
            P("req"),
            P("req", "hid"),
            P("req", "hid"),
            P("hid", "req"),
        ),
        out_specs=P("hid", "req"),
        check_vma=False,
    )
```

```python
import jax
import jax.numpy as jnp
from jax import lax
from jax.experimental import pallas as pl
from jax.experimental.pallas import tpu as pltpu
from jax.sharding import PartitionSpec as P

D = 8192
KVH = 8
HD = 128
PREFIX = 8192
PBLK = 256


ROPE_BASE = 500000.0
EPSILON = 1e-05
MASKED = -1e30


def rotate(vectors, positions):
    half_width = vectors.shape[-1] // 2
    exponent = 2.0 * jnp.arange(half_width, dtype=jnp.float32) / vectors.shape[-1]
    frequency = jnp.exp(-jnp.log(ROPE_BASE) * exponent)
    angles = positions[..., None] * frequency
    cosine = jnp.cos(angles)
    sine_part = jnp.sin(angles)
    lower_half = vectors[..., :half_width]
    upper_half = vectors[..., half_width:]
    return jnp.concatenate(
        [
            lower_half * cosine - upper_half * sine_part,
            upper_half * cosine + lower_half * sine_part,
        ],
        axis=-1,
    )


def slot_lengths(suffix_len, slot_request):
    total_count = suffix_len.shape[0]
    matches = (slot_request[:, None] == jnp.arange(total_count, dtype=jnp.int32)[None, :]).astype(
        jnp.int32
    )
    return jnp.sum(matches * suffix_len[None, :], axis=1)


def token_source(suffix_len, slot_request, tokens, maxlen):
    total_count = suffix_len.shape[0]
    numbers = jnp.arange(total_count, dtype=jnp.int32)
    starts = jnp.cumsum(suffix_len) - suffix_len
    token_ids = jnp.arange(tokens, dtype=jnp.int32)
    reached = (token_ids[:, None] >= starts[None, :]).astype(jnp.int32)
    owner_req = jnp.sum(reached, axis=1) - 1
    onehot = (owner_req[:, None] == numbers[None, :]).astype(jnp.int32)
    start_tok = jnp.sum(onehot * starts[None, :], axis=1)
    inverse = jnp.sum(
        (slot_request[:, None] == numbers[None, :]).astype(jnp.int32) * numbers[:, None], axis=0
    )
    slot_tok = jnp.sum(onehot * inverse[None, :], axis=1)
    return slot_tok * maxlen + token_ids - start_tok


def merge_states(state_one, state_two):
    max_one, total_one, acc_one = state_one
    max_two, total_two, acc_two = state_two
    new_max = jnp.maximum(max_one, max_two)
    shrink_one = jnp.exp(max_one - new_max)
    shrink_two = jnp.exp(max_two - new_max)
    new_total = total_one * shrink_one + total_two * shrink_two
    new_acc = acc_one * shrink_one[:, None] + acc_two * shrink_two[:, None]
    return (new_max, new_total, new_acc)


def exchange_sum(values, axis, count):
    parts = lax.all_to_all(
        values.reshape(count, values.shape[0] // count, values.shape[1]), axis, 0, 0, tiled=True
    )
    return jnp.sum(parts.astype(jnp.float32), axis=0)


def exchange_gather(values, axis, count):
    parts = lax.all_to_all(
        jnp.broadcast_to(values[None], (count,) + values.shape), axis, 0, 0, tiled=True
    )
    return parts.reshape(count * values.shape[0], values.shape[1])


def prefix_kernel(q_ref, k_ref, v_ref, m_ref, l_ref, acc_ref):
    @pl.when(pl.program_id(1) == 0)
    def _():
        m_ref[...] = jnp.full(m_ref.shape, MASKED, jnp.float32)
        l_ref[...] = jnp.zeros(l_ref.shape, jnp.float32)
        acc_ref[...] = jnp.zeros(acc_ref.shape, jnp.float32)

    scores = lax.dot_general(
        q_ref[...], k_ref[...], (((1,), (1,)), ((), ())), preferred_element_type=jnp.float32
    ) * (HD ** (-0.5))
    m_prev = m_ref[...]
    m_new = jnp.maximum(m_prev, jnp.max(scores, axis=1, keepdims=True))
    shrink = jnp.exp(m_prev - m_new)
    probs = jnp.exp(scores - m_new)
    l_ref[...] = shrink * l_ref[...] + jnp.sum(probs, axis=1, keepdims=True)
    acc_ref[...] = shrink * acc_ref[...] + jnp.dot(
        probs.astype(jnp.bfloat16), v_ref[...], preferred_element_type=jnp.float32
    )
    m_ref[...] = m_new


def prefix_attention(query_flat, keys_values, q_tile=512, k_tile=4096):
    rows = query_flat.shape[0]
    length = keys_values.shape[0]
    return pl.pallas_call(
        prefix_kernel,
        out_shape=(
            jax.ShapeDtypeStruct((rows, 1), jnp.float32),
            jax.ShapeDtypeStruct((rows, 1), jnp.float32),
            jax.ShapeDtypeStruct((rows, HD), jnp.float32),
        ),
        grid=(rows // q_tile, length // k_tile),
        in_specs=[
            pl.BlockSpec((q_tile, HD), lambda i, j: (i, 0)),
            pl.BlockSpec((k_tile, HD), lambda i, j: (j, 0)),
            pl.BlockSpec((k_tile, HD), lambda i, j: (j, 1)),
        ],
        out_specs=(
            pl.BlockSpec((q_tile, 1), lambda i, j: (i, 0)),
            pl.BlockSpec((q_tile, 1), lambda i, j: (i, 0)),
            pl.BlockSpec((q_tile, HD), lambda i, j: (i, 0)),
        ),
        compiler_params=pltpu.CompilerParams(dimension_semantics=("parallel", "arbitrary")),
    )(query_flat, keys_values, keys_values)


def on_device(
    queries,
    suffix_keys,
    suffix_values,
    prefix_cache,
    prefix_block,
    suffix_len,
    slot_request,
    residual,
    out_weight,
    post_gain,
    gate_weight,
    up_weight,
    down_weight,
):
    hid_count = lax.axis_size("hid")
    req_count = lax.axis_size("req")
    req_index = lax.axis_index("req")
    hid_index = lax.axis_index("hid")
    local_slots, maxlen, query_cols = queries.shape
    head_count = query_cols // HD
    kv_head = hid_index // (hid_count // KVH)
    scale = HD ** (-0.5)
    all_rows = local_slots * maxlen * head_count
    places = jnp.arange(maxlen, dtype=jnp.int32)
    suffix_pos = (PREFIX + places).astype(jnp.float32)
    query_rot = rotate(
        queries.astype(jnp.float32).reshape(local_slots, maxlen, head_count, HD),
        suffix_pos[None, :, None],
    ).astype(jnp.bfloat16)
    key_cols = lax.dynamic_slice_in_dim(suffix_keys, kv_head * HD, HD, 2)
    key_rot = rotate(key_cols.astype(jnp.float32), suffix_pos[None, :]).astype(jnp.bfloat16)
    value_cols = lax.dynamic_slice_in_dim(suffix_values, kv_head * HD, HD, 2)
    lengths_all = slot_lengths(suffix_len, slot_request)
    local_len = lax.dynamic_slice_in_dim(lengths_all, req_index * local_slots, local_slots, 0)
    allowed = (places[None, :, None] >= places[None, None, :]) & (
        places[None, None, :] < local_len[:, None, None]
    )
    suffix_scores = (
        jnp.einsum("jthd,jud->jthu", query_rot, key_rot, preferred_element_type=jnp.float32) * scale
    )
    suffix_scores = jnp.where(allowed[:, :, None, :], suffix_scores, MASKED)
    suffix_max = jnp.max(suffix_scores, axis=-1)
    suffix_prob = jnp.exp(suffix_scores - suffix_max[..., None])
    suffix_total = jnp.sum(suffix_prob, axis=-1)
    suffix_acc = jnp.einsum(
        "jthu,jud->jthd",
        suffix_prob.astype(jnp.bfloat16),
        value_cols,
        preferred_element_type=jnp.float32,
    )
    suffix_state = (
        suffix_max.reshape(all_rows),
        suffix_total.reshape(all_rows),
        suffix_acc.reshape(all_rows, HD),
    )
    local_prefix = prefix_cache.shape[0]
    block_count = prefix_block.shape[0]
    row_ids = req_index * local_prefix + jnp.arange(local_prefix, dtype=jnp.int32)
    block_match = (
        (row_ids // PBLK)[:, None] == jnp.arange(block_count, dtype=jnp.int32)[None, :]
    ).astype(jnp.int32)
    logical_block = jnp.sum(block_match * prefix_block[None, :], axis=1)
    pre_pos = (logical_block * PBLK + row_ids % PBLK).astype(jnp.float32)
    key_block = lax.dynamic_slice(prefix_cache, (0, 0, kv_head * HD), (local_prefix, 1, HD))
    pre_keys = rotate(key_block.reshape(local_prefix, HD).astype(jnp.float32), pre_pos).astype(
        jnp.bfloat16
    )
    value_block = lax.dynamic_slice(prefix_cache, (0, 1, kv_head * HD), (local_prefix, 1, HD))
    pre_values = value_block.reshape(local_prefix, HD)
    query_flat = query_rot.reshape(all_rows, HD)
    keys_values = lax.all_gather(
        jnp.concatenate([pre_keys, pre_values], axis=1), "req", axis=0, tiled=True
    )
    new_max, new_total, new_acc = prefix_attention(query_flat, keys_values)
    final_state = (new_max.reshape(all_rows), new_total.reshape(all_rows), new_acc)
    final_state = merge_states(final_state, suffix_state)
    final_max, final_total, final_acc = final_state
    attn_local = (
        (final_acc / final_total[:, None])
        .astype(jnp.bfloat16)
        .reshape(local_slots * maxlen, head_count * HD)
    )
    tokens = residual.shape[0]
    own_rows = tokens // hid_count
    source = token_source(suffix_len, slot_request, tokens, maxlen)
    token_rows = jnp.take(lax.all_gather(attn_local, "req", axis=0, tiled=True), source, axis=0)
    projected = jnp.dot(token_rows, out_weight, preferred_element_type=jnp.float32)
    summed = exchange_sum(projected.astype(jnp.bfloat16), "hid", hid_count)
    residual_own = lax.dynamic_slice_in_dim(residual, hid_index * own_rows, own_rows, 0)
    resid_own = (residual_own.astype(jnp.float32) + summed).astype(jnp.bfloat16)
    resid_all = exchange_gather(resid_own, "hid", hid_count)
    resid_f = lax.optimization_barrier(resid_all).astype(jnp.float32)
    squares = jnp.sum(resid_f * resid_f, axis=1)
    scaled = (resid_f * post_gain[None, :]).astype(jnp.bfloat16)
    gate_part = jnp.dot(scaled, gate_weight, preferred_element_type=jnp.float32)
    up_part = jnp.dot(scaled, up_weight, preferred_element_type=jnp.float32)
    square_all = lax.psum(squares, "req")
    ff_cols = gate_part.shape[1]
    both_sum = lax.psum_scatter(
        jnp.concatenate([gate_part.astype(jnp.bfloat16), up_part.astype(jnp.bfloat16)], axis=1),
        "req",
        scatter_dimension=0,
        tiled=True,
    ).astype(jnp.float32)
    gate_sum, up_sum = both_sum[:, :ff_cols], both_sum[:, ff_cols:]
    row_count = tokens // req_count
    square_sum = lax.dynamic_slice_in_dim(square_all, req_index * row_count, row_count, 0)
    inv_rms = lax.rsqrt(square_sum / D + EPSILON)
    hidden = (jax.nn.silu(gate_sum * inv_rms[:, None]) * (up_sum * inv_rms[:, None])).astype(
        jnp.bfloat16
    )
    hidden_all = lax.all_gather(hidden, "req", axis=0, tiled=True)
    mixed_rows = exchange_sum(
        jnp.dot(hidden_all, down_weight, preferred_element_type=jnp.float32).astype(jnp.bfloat16),
        "hid",
        hid_count,
    )
    return (resid_own.astype(jnp.float32) + mixed_rows).astype(jnp.bfloat16)


def solution(mesh):
    return jax.shard_map(
        on_device,
        mesh=mesh,
        in_specs=(
            P("req", None, "hid"),
            P("req", None, None),
            P("req", None, None),
            P("req", None, None),
            P(),
            P(),
            P(),
            P(None, "req"),
            P("hid", "req"),
            P("req"),
            P("req", "hid"),
            P("req", "hid"),
            P("hid", "req"),
        ),
        out_specs=P("hid", "req"),
        check_vma=False,
    )
```

```python
import jax
import jax.numpy as jnp
from jax import lax
from jax.experimental import pallas as pl
from jax.experimental.pallas import tpu as pltpu
from jax.sharding import PartitionSpec as P

D = 8192
KVH = 8
HD = 128
PREFIX = 8192
PBLK = 256


ROPE_BASE = 500000.0
EPSILON = 1e-05
MASKED = -1e30


def rotate(vectors, positions):
    half_width = vectors.shape[-1] // 2
    exponent = 2.0 * jnp.arange(half_width, dtype=jnp.float32) / vectors.shape[-1]
    frequency = jnp.exp(-jnp.log(ROPE_BASE) * exponent)
    angles = positions[..., None] * frequency
    cosine = jnp.cos(angles)
    sine_part = jnp.sin(angles)
    lower_half = vectors[..., :half_width]
    upper_half = vectors[..., half_width:]
    return jnp.concatenate(
        [
            lower_half * cosine - upper_half * sine_part,
            upper_half * cosine + lower_half * sine_part,
        ],
        axis=-1,
    )


def slot_lengths(suffix_len, slot_request):
    total_count = suffix_len.shape[0]
    matches = (slot_request[:, None] == jnp.arange(total_count, dtype=jnp.int32)[None, :]).astype(
        jnp.int32
    )
    return jnp.sum(matches * suffix_len[None, :], axis=1)


def token_source(suffix_len, slot_request, tokens, maxlen):
    total_count = suffix_len.shape[0]
    numbers = jnp.arange(total_count, dtype=jnp.int32)
    starts = jnp.cumsum(suffix_len) - suffix_len
    token_ids = jnp.arange(tokens, dtype=jnp.int32)
    reached = (token_ids[:, None] >= starts[None, :]).astype(jnp.int32)
    owner_req = jnp.sum(reached, axis=1) - 1
    onehot = (owner_req[:, None] == numbers[None, :]).astype(jnp.int32)
    start_tok = jnp.sum(onehot * starts[None, :], axis=1)
    inverse = jnp.sum(
        (slot_request[:, None] == numbers[None, :]).astype(jnp.int32) * numbers[:, None], axis=0
    )
    slot_tok = jnp.sum(onehot * inverse[None, :], axis=1)
    return slot_tok * maxlen + token_ids - start_tok


def merge_states(state_one, state_two):
    max_one, total_one, acc_one = state_one
    max_two, total_two, acc_two = state_two
    new_max = jnp.maximum(max_one, max_two)
    shrink_one = jnp.exp(max_one - new_max)
    shrink_two = jnp.exp(max_two - new_max)
    new_total = total_one * shrink_one + total_two * shrink_two
    new_acc = acc_one * shrink_one[:, None] + acc_two * shrink_two[:, None]
    return (new_max, new_total, new_acc)


def exchange_sum(values, axis, count):
    parts = lax.all_to_all(
        values.reshape(count, values.shape[0] // count, values.shape[1]), axis, 0, 0, tiled=True
    )
    return jnp.sum(parts.astype(jnp.float32), axis=0)


def exchange_gather(values, axis, count):
    parts = lax.all_to_all(
        jnp.broadcast_to(values[None], (count,) + values.shape), axis, 0, 0, tiled=True
    )
    return parts.reshape(count * values.shape[0], values.shape[1])


def prefix_kernel(q_ref, k_ref, v_ref, m_ref, l_ref, acc_ref):
    @pl.when(pl.program_id(1) == 0)
    def _():
        m_ref[...] = jnp.full(m_ref.shape, MASKED, jnp.float32)
        l_ref[...] = jnp.zeros(l_ref.shape, jnp.float32)
        acc_ref[...] = jnp.zeros(acc_ref.shape, jnp.float32)

    scores = lax.dot_general(
        q_ref[...], k_ref[...], (((1,), (1,)), ((), ())), preferred_element_type=jnp.float32
    ) * (HD ** (-0.5))
    m_prev = m_ref[...]
    m_new = jnp.maximum(m_prev, jnp.max(scores, axis=1, keepdims=True))
    shrink = jnp.exp(m_prev - m_new)
    probs = jnp.exp(scores - m_new)
    l_ref[...] = shrink * l_ref[...] + jnp.sum(probs, axis=1, keepdims=True)
    acc_ref[...] = shrink * acc_ref[...] + jnp.dot(
        probs.astype(jnp.bfloat16), v_ref[...], preferred_element_type=jnp.float32
    )
    m_ref[...] = m_new


def prefix_attention(query_flat, keys_values, q_tile=512, k_tile=4096):
    rows = query_flat.shape[0]
    length = keys_values.shape[0]
    return pl.pallas_call(
        prefix_kernel,
        out_shape=(
            jax.ShapeDtypeStruct((rows, 1), jnp.float32),
            jax.ShapeDtypeStruct((rows, 1), jnp.float32),
            jax.ShapeDtypeStruct((rows, HD), jnp.float32),
        ),
        grid=(rows // q_tile, length // k_tile),
        in_specs=[
            pl.BlockSpec((q_tile, HD), lambda i, j: (i, 0)),
            pl.BlockSpec((k_tile, HD), lambda i, j: (j, 0)),
            pl.BlockSpec((k_tile, HD), lambda i, j: (j, 1)),
        ],
        out_specs=(
            pl.BlockSpec((q_tile, 1), lambda i, j: (i, 0)),
            pl.BlockSpec((q_tile, 1), lambda i, j: (i, 0)),
            pl.BlockSpec((q_tile, HD), lambda i, j: (i, 0)),
        ),
        compiler_params=pltpu.CompilerParams(dimension_semantics=("parallel", "arbitrary")),
    )(query_flat, keys_values, keys_values)


def on_device(
    queries,
    suffix_keys,
    suffix_values,
    prefix_cache,
    prefix_block,
    suffix_len,
    slot_request,
    residual,
    out_weight,
    post_gain,
    gate_weight,
    up_weight,
    down_weight,
):
    hid_count = lax.axis_size("hid")
    req_count = lax.axis_size("req")
    req_index = lax.axis_index("req")
    hid_index = lax.axis_index("hid")
    local_slots, maxlen, query_cols = queries.shape
    head_count = query_cols // HD
    kv_head = hid_index // (hid_count // KVH)
    scale = HD ** (-0.5)
    all_rows = local_slots * maxlen * head_count
    places = jnp.arange(maxlen, dtype=jnp.int32)
    suffix_pos = (PREFIX + places).astype(jnp.float32)
    query_rot = rotate(
        queries.astype(jnp.float32).reshape(local_slots, maxlen, head_count, HD),
        suffix_pos[None, :, None],
    ).astype(jnp.bfloat16)
    key_cols = lax.dynamic_slice_in_dim(suffix_keys, kv_head * HD, HD, 2)
    key_rot = rotate(key_cols.astype(jnp.float32), suffix_pos[None, :]).astype(jnp.bfloat16)
    value_cols = lax.dynamic_slice_in_dim(suffix_values, kv_head * HD, HD, 2)
    lengths_all = slot_lengths(suffix_len, slot_request)
    local_len = lax.dynamic_slice_in_dim(lengths_all, req_index * local_slots, local_slots, 0)
    allowed = (places[None, :, None] >= places[None, None, :]) & (
        places[None, None, :] < local_len[:, None, None]
    )
    suffix_scores = (
        jnp.einsum("jthd,jud->jthu", query_rot, key_rot, preferred_element_type=jnp.float32) * scale
    )
    suffix_scores = jnp.where(allowed[:, :, None, :], suffix_scores, MASKED)
    suffix_max = jnp.max(suffix_scores, axis=-1)
    suffix_prob = jnp.exp(suffix_scores - suffix_max[..., None])
    suffix_total = jnp.sum(suffix_prob, axis=-1)
    suffix_acc = jnp.einsum(
        "jthu,jud->jthd",
        suffix_prob.astype(jnp.bfloat16),
        value_cols,
        preferred_element_type=jnp.float32,
    )
    suffix_state = (
        suffix_max.reshape(all_rows),
        suffix_total.reshape(all_rows),
        suffix_acc.reshape(all_rows, HD),
    )
    local_prefix = prefix_cache.shape[0]
    block_count = prefix_block.shape[0]
    row_ids = req_index * local_prefix + jnp.arange(local_prefix, dtype=jnp.int32)
    block_match = (
        (row_ids // PBLK)[:, None] == jnp.arange(block_count, dtype=jnp.int32)[None, :]
    ).astype(jnp.int32)
    logical_block = jnp.sum(block_match * prefix_block[None, :], axis=1)
    pre_pos = (logical_block * PBLK + row_ids % PBLK).astype(jnp.float32)
    key_block = lax.dynamic_slice(prefix_cache, (0, 0, kv_head * HD), (local_prefix, 1, HD))
    pre_keys = rotate(key_block.reshape(local_prefix, HD).astype(jnp.float32), pre_pos).astype(
        jnp.bfloat16
    )
    value_block = lax.dynamic_slice(prefix_cache, (0, 1, kv_head * HD), (local_prefix, 1, HD))
    pre_values = value_block.reshape(local_prefix, HD)
    query_flat = query_rot.reshape(all_rows, HD)
    keys_values = lax.all_gather(
        jnp.concatenate([pre_keys, pre_values], axis=1), "req", axis=0, tiled=True
    )
    new_max, new_total, new_acc = prefix_attention(query_flat, keys_values)
    final_state = (new_max.reshape(all_rows), new_total.reshape(all_rows), new_acc)
    final_state = merge_states(final_state, suffix_state)
    final_max, final_total, final_acc = final_state
    attn_local = (
        (final_acc / final_total[:, None])
        .astype(jnp.bfloat16)
        .reshape(local_slots * maxlen, head_count * HD)
    )
    tokens = residual.shape[0]
    own_rows = tokens // hid_count
    source = token_source(suffix_len, slot_request, tokens, maxlen)
    attn_all = lax.all_gather(attn_local, "req", axis=0, tiled=True)
    pick = (source[:, None] == jnp.arange(attn_all.shape[0], dtype=jnp.int32)[None, :]).astype(
        jnp.bfloat16
    )
    token_rows = jnp.dot(pick, attn_all, preferred_element_type=jnp.float32).astype(jnp.bfloat16)
    projected = jnp.dot(token_rows, out_weight, preferred_element_type=jnp.float32)
    summed = exchange_sum(projected.astype(jnp.bfloat16), "hid", hid_count)
    residual_own = lax.dynamic_slice_in_dim(residual, hid_index * own_rows, own_rows, 0)
    resid_own = (residual_own.astype(jnp.float32) + summed).astype(jnp.bfloat16)
    resid_all = exchange_gather(resid_own, "hid", hid_count)
    resid_f = lax.optimization_barrier(resid_all).astype(jnp.float32)
    squares = jnp.sum(resid_f * resid_f, axis=1)
    scaled = (resid_f * post_gain[None, :]).astype(jnp.bfloat16)
    gate_part = jnp.dot(scaled, gate_weight, preferred_element_type=jnp.float32)
    up_part = jnp.dot(scaled, up_weight, preferred_element_type=jnp.float32)
    square_all = lax.psum(squares, "req")
    ff_cols = gate_part.shape[1]
    both_sum = lax.psum_scatter(
        jnp.concatenate([gate_part.astype(jnp.bfloat16), up_part.astype(jnp.bfloat16)], axis=1),
        "req",
        scatter_dimension=0,
        tiled=True,
    ).astype(jnp.float32)
    gate_sum, up_sum = both_sum[:, :ff_cols], both_sum[:, ff_cols:]
    row_count = tokens // req_count
    square_sum = lax.dynamic_slice_in_dim(square_all, req_index * row_count, row_count, 0)
    inv_rms = lax.rsqrt(square_sum / D + EPSILON)
    hidden = (jax.nn.silu(gate_sum * inv_rms[:, None]) * (up_sum * inv_rms[:, None])).astype(
        jnp.bfloat16
    )
    hidden_all = lax.all_gather(hidden, "req", axis=0, tiled=True)
    mixed_rows = exchange_sum(
        jnp.dot(hidden_all, down_weight, preferred_element_type=jnp.float32).astype(jnp.bfloat16),
        "hid",
        hid_count,
    )
    return (resid_own.astype(jnp.float32) + mixed_rows).astype(jnp.bfloat16)


def solution(mesh):
    return jax.shard_map(
        on_device,
        mesh=mesh,
        in_specs=(
            P("req", None, "hid"),
            P("req", None, None),
            P("req", None, None),
            P("req", None, None),
            P(),
            P(),
            P(),
            P(None, "req"),
            P("hid", "req"),
            P("req"),
            P("req", "hid"),
            P("req", "hid"),
            P("hid", "req"),
        ),
        out_specs=P("hid", "req"),
        check_vma=False,
    )
```

```python
import jax
import jax.numpy as jnp
from jax import lax
from jax.experimental import pallas as pl
from jax.experimental.pallas import tpu as pltpu
from jax.sharding import PartitionSpec as P

D = 8192
KVH = 8
HD = 128
PREFIX = 8192
PBLK = 256


ROPE_BASE = 500000.0
EPSILON = 1e-05
MASKED = -1e30


def rotate(vectors, positions):
    half_width = vectors.shape[-1] // 2
    exponent = 2.0 * jnp.arange(half_width, dtype=jnp.float32) / vectors.shape[-1]
    frequency = jnp.exp(-jnp.log(ROPE_BASE) * exponent)
    angles = positions[..., None] * frequency
    cosine = jnp.cos(angles)
    sine_part = jnp.sin(angles)
    lower_half = vectors[..., :half_width]
    upper_half = vectors[..., half_width:]
    return jnp.concatenate(
        [
            lower_half * cosine - upper_half * sine_part,
            upper_half * cosine + lower_half * sine_part,
        ],
        axis=-1,
    )


def slot_lengths(suffix_len, slot_request):
    total_count = suffix_len.shape[0]
    matches = (slot_request[:, None] == jnp.arange(total_count, dtype=jnp.int32)[None, :]).astype(
        jnp.int32
    )
    return jnp.sum(matches * suffix_len[None, :], axis=1)


def token_source(suffix_len, slot_request, tokens, maxlen):
    total_count = suffix_len.shape[0]
    numbers = jnp.arange(total_count, dtype=jnp.int32)
    starts = jnp.cumsum(suffix_len) - suffix_len
    token_ids = jnp.arange(tokens, dtype=jnp.int32)
    reached = (token_ids[:, None] >= starts[None, :]).astype(jnp.int32)
    owner_req = jnp.sum(reached, axis=1) - 1
    onehot = (owner_req[:, None] == numbers[None, :]).astype(jnp.int32)
    start_tok = jnp.sum(onehot * starts[None, :], axis=1)
    inverse = jnp.sum(
        (slot_request[:, None] == numbers[None, :]).astype(jnp.int32) * numbers[:, None], axis=0
    )
    slot_tok = jnp.sum(onehot * inverse[None, :], axis=1)
    return slot_tok * maxlen + token_ids - start_tok


def merge_states(state_one, state_two):
    max_one, total_one, acc_one = state_one
    max_two, total_two, acc_two = state_two
    new_max = jnp.maximum(max_one, max_two)
    shrink_one = jnp.exp(max_one - new_max)
    shrink_two = jnp.exp(max_two - new_max)
    new_total = total_one * shrink_one + total_two * shrink_two
    new_acc = acc_one * shrink_one[:, None] + acc_two * shrink_two[:, None]
    return (new_max, new_total, new_acc)


def exchange_sum(values, axis, count):
    parts = lax.all_to_all(
        values.reshape(count, values.shape[0] // count, values.shape[1]), axis, 0, 0, tiled=True
    )
    return jnp.sum(parts.astype(jnp.float32), axis=0)


def exchange_gather(values, axis, count):
    parts = lax.all_to_all(
        jnp.broadcast_to(values[None], (count,) + values.shape), axis, 0, 0, tiled=True
    )
    return parts.reshape(count * values.shape[0], values.shape[1])


def prefix_kernel(q_ref, k_ref, v_ref, m_ref, l_ref, acc_ref):
    @pl.when(pl.program_id(1) == 0)
    def _():
        m_ref[...] = jnp.full(m_ref.shape, MASKED, jnp.float32)
        l_ref[...] = jnp.zeros(l_ref.shape, jnp.float32)
        acc_ref[...] = jnp.zeros(acc_ref.shape, jnp.float32)

    scores = lax.dot_general(
        q_ref[...], k_ref[...], (((1,), (1,)), ((), ())), preferred_element_type=jnp.float32
    ) * (HD ** (-0.5))
    m_prev = m_ref[...]
    m_new = jnp.maximum(m_prev, jnp.max(scores, axis=1, keepdims=True))
    shrink = jnp.exp(m_prev - m_new)
    probs = jnp.exp(scores - m_new)
    l_ref[...] = shrink * l_ref[...] + jnp.sum(probs, axis=1, keepdims=True)
    acc_ref[...] = shrink * acc_ref[...] + jnp.dot(
        probs.astype(jnp.bfloat16), v_ref[...], preferred_element_type=jnp.float32
    )
    m_ref[...] = m_new


def prefix_attention(query_flat, keys_values, q_tile=1024, k_tile=4096):
    rows = query_flat.shape[0]
    length = keys_values.shape[0]
    return pl.pallas_call(
        prefix_kernel,
        out_shape=(
            jax.ShapeDtypeStruct((rows, 1), jnp.float32),
            jax.ShapeDtypeStruct((rows, 1), jnp.float32),
            jax.ShapeDtypeStruct((rows, HD), jnp.float32),
        ),
        grid=(rows // q_tile, length // k_tile),
        in_specs=[
            pl.BlockSpec((q_tile, HD), lambda i, j: (i, 0)),
            pl.BlockSpec((k_tile, HD), lambda i, j: (j, 0)),
            pl.BlockSpec((k_tile, HD), lambda i, j: (j, 1)),
        ],
        out_specs=(
            pl.BlockSpec((q_tile, 1), lambda i, j: (i, 0)),
            pl.BlockSpec((q_tile, 1), lambda i, j: (i, 0)),
            pl.BlockSpec((q_tile, HD), lambda i, j: (i, 0)),
        ),
        compiler_params=pltpu.CompilerParams(dimension_semantics=("parallel", "arbitrary")),
    )(query_flat, keys_values, keys_values)


def on_device(
    queries,
    suffix_keys,
    suffix_values,
    prefix_cache,
    prefix_block,
    suffix_len,
    slot_request,
    residual,
    out_weight,
    post_gain,
    gate_weight,
    up_weight,
    down_weight,
):
    hid_count = lax.axis_size("hid")
    req_count = lax.axis_size("req")
    req_index = lax.axis_index("req")
    hid_index = lax.axis_index("hid")
    local_slots, maxlen, query_cols = queries.shape
    head_count = query_cols // HD
    kv_head = hid_index // (hid_count // KVH)
    scale = HD ** (-0.5)
    all_rows = local_slots * maxlen * head_count
    places = jnp.arange(maxlen, dtype=jnp.int32)
    suffix_pos = (PREFIX + places).astype(jnp.float32)
    query_rot = rotate(
        queries.astype(jnp.float32).reshape(local_slots, maxlen, head_count, HD),
        suffix_pos[None, :, None],
    ).astype(jnp.bfloat16)
    key_cols = lax.dynamic_slice_in_dim(suffix_keys, kv_head * HD, HD, 2)
    key_rot = rotate(key_cols.astype(jnp.float32), suffix_pos[None, :]).astype(jnp.bfloat16)
    value_cols = lax.dynamic_slice_in_dim(suffix_values, kv_head * HD, HD, 2)
    lengths_all = slot_lengths(suffix_len, slot_request)
    local_len = lax.dynamic_slice_in_dim(lengths_all, req_index * local_slots, local_slots, 0)
    allowed = (places[None, :, None] >= places[None, None, :]) & (
        places[None, None, :] < local_len[:, None, None]
    )
    suffix_scores = (
        jnp.einsum("jthd,jud->jthu", query_rot, key_rot, preferred_element_type=jnp.float32) * scale
    )
    suffix_scores = jnp.where(allowed[:, :, None, :], suffix_scores, MASKED)
    suffix_max = jnp.max(suffix_scores, axis=-1)
    suffix_prob = jnp.exp(suffix_scores - suffix_max[..., None])
    suffix_total = jnp.sum(suffix_prob, axis=-1)
    suffix_acc = jnp.einsum(
        "jthu,jud->jthd",
        suffix_prob.astype(jnp.bfloat16),
        value_cols,
        preferred_element_type=jnp.float32,
    )
    suffix_state = (
        suffix_max.reshape(all_rows),
        suffix_total.reshape(all_rows),
        suffix_acc.reshape(all_rows, HD),
    )
    local_prefix = prefix_cache.shape[0]
    block_count = prefix_block.shape[0]
    row_ids = req_index * local_prefix + jnp.arange(local_prefix, dtype=jnp.int32)
    block_match = (
        (row_ids // PBLK)[:, None] == jnp.arange(block_count, dtype=jnp.int32)[None, :]
    ).astype(jnp.int32)
    logical_block = jnp.sum(block_match * prefix_block[None, :], axis=1)
    pre_pos = (logical_block * PBLK + row_ids % PBLK).astype(jnp.float32)
    key_block = lax.dynamic_slice(prefix_cache, (0, 0, kv_head * HD), (local_prefix, 1, HD))
    pre_keys = rotate(key_block.reshape(local_prefix, HD).astype(jnp.float32), pre_pos).astype(
        jnp.bfloat16
    )
    value_block = lax.dynamic_slice(prefix_cache, (0, 1, kv_head * HD), (local_prefix, 1, HD))
    pre_values = value_block.reshape(local_prefix, HD)
    query_flat = query_rot.reshape(all_rows, HD)
    keys_values = lax.all_gather(
        jnp.concatenate([pre_keys, pre_values], axis=1), "req", axis=0, tiled=True
    )
    new_max, new_total, new_acc = prefix_attention(query_flat, keys_values)
    final_state = (new_max.reshape(all_rows), new_total.reshape(all_rows), new_acc)
    final_state = merge_states(final_state, suffix_state)
    final_max, final_total, final_acc = final_state
    attn_local = (
        (final_acc / final_total[:, None])
        .astype(jnp.bfloat16)
        .reshape(local_slots * maxlen, head_count * HD)
    )
    tokens = residual.shape[0]
    own_rows = tokens // hid_count
    source = token_source(suffix_len, slot_request, tokens, maxlen)
    attn_all = lax.all_gather(attn_local, "req", axis=0, tiled=True)
    pick = (source[:, None] == jnp.arange(attn_all.shape[0], dtype=jnp.int32)[None, :]).astype(
        jnp.bfloat16
    )
    token_rows = jnp.dot(pick, attn_all, preferred_element_type=jnp.float32).astype(jnp.bfloat16)
    projected = jnp.dot(token_rows, out_weight, preferred_element_type=jnp.float32)
    summed = exchange_sum(projected.astype(jnp.bfloat16), "hid", hid_count)
    residual_own = lax.dynamic_slice_in_dim(residual, hid_index * own_rows, own_rows, 0)
    resid_own = (residual_own.astype(jnp.float32) + summed).astype(jnp.bfloat16)
    resid_all = exchange_gather(resid_own, "hid", hid_count)
    resid_f = lax.optimization_barrier(resid_all).astype(jnp.float32)
    squares = jnp.sum(resid_f * resid_f, axis=1)
    scaled = (resid_f * post_gain[None, :]).astype(jnp.bfloat16)
    gate_part = jnp.dot(scaled, gate_weight, preferred_element_type=jnp.float32)
    up_part = jnp.dot(scaled, up_weight, preferred_element_type=jnp.float32)
    square_all = lax.psum(squares, "req")
    ff_cols = gate_part.shape[1]
    both_sum = lax.psum_scatter(
        jnp.concatenate([gate_part.astype(jnp.bfloat16), up_part.astype(jnp.bfloat16)], axis=1),
        "req",
        scatter_dimension=0,
        tiled=True,
    ).astype(jnp.float32)
    gate_sum, up_sum = both_sum[:, :ff_cols], both_sum[:, ff_cols:]
    row_count = tokens // req_count
    square_sum = lax.dynamic_slice_in_dim(square_all, req_index * row_count, row_count, 0)
    inv_rms = lax.rsqrt(square_sum / D + EPSILON)
    hidden = (jax.nn.silu(gate_sum * inv_rms[:, None]) * (up_sum * inv_rms[:, None])).astype(
        jnp.bfloat16
    )
    hidden_all = lax.all_gather(hidden, "req", axis=0, tiled=True)
    mixed_rows = exchange_sum(
        jnp.dot(hidden_all, down_weight, preferred_element_type=jnp.float32).astype(jnp.bfloat16),
        "hid",
        hid_count,
    )
    return (resid_own.astype(jnp.float32) + mixed_rows).astype(jnp.bfloat16)


def solution(mesh):
    return jax.shard_map(
        on_device,
        mesh=mesh,
        in_specs=(
            P("req", None, "hid"),
            P("req", None, None),
            P("req", None, None),
            P("req", None, None),
            P(),
            P(),
            P(),
            P(None, "req"),
            P("hid", "req"),
            P("req"),
            P("req", "hid"),
            P("req", "hid"),
            P("hid", "req"),
        ),
        out_specs=P("hid", "req"),
        check_vma=False,
    )
```
